128 devices in a mesh: dp: 8 (over z, core), ctx: 16 (over x, y).
Axes of the slice: x: 4, y: 4, z: 4, core: 2. Of those that a mesh axis runs over, the one named last changes fastest.
Arguments:
- query_input: bfloat16 [8, 2048, 8192], P('dp', 'ctx'), may hold values from -12 to 12
- key_input: bfloat16 [8, 2048, 1024], P('dp', 'ctx'), may hold values from -12 to 12
- value_input: bfloat16 [8, 2048, 1024], P('dp', 'ctx'), may hold values from -6 to 6
- out_grad: bfloat16 [8, 2048, 8192], P('dp', 'ctx'), may hold values from -6 to 6
- query_bias: float32 [8192], replicated, may hold values from -1.75 to 1.75
- key_bias: float32 [1024], replicated, may hold values from -1.75 to 1.75
- value_bias: float32 [1024], replicated, may hold values from -1.75 to 1.75
- parents: int32 [8, 16], P('dp'), may hold values from 0 to 14, as said below
Outputs:
- attended: bfloat16 [8, 2048, 8192], P('dp', 'ctx')
- query_grad: float32 [8, 2048, 8192], P('dp', 'ctx')
- key_grad: float32 [8, 2048, 1024], P('dp', 'ctx')
- value_grad: float32 [8, 2048, 1024], P('dp', 'ctx')
- query_bias_grad: float32 [8192], replicated
- key_bias_grad: float32 [1024], replicated
- value_bias_grad: float32 [1024], replicated
The draws below stay inside these ranges and needn't reach their ends.
Inputs may be any that keep to these rules, and one draw needn't show every extreme that they name: parents[t, 0] = 0 marks the root block; every other block's parent is an earlier block; the last block's parent is the block before it.
All inputs are finite; a program needn't handle non-finite values.
Results may differ from the reference program's by a relative error of at most 0.028.
Values may be sent and summed in bfloat16 or wider, within the bound.
No kernel may reach another device: no remote copies, remote signals or barrier semaphores. Data moves between devices by JAX's collectives and lax.ppermute only.
A program may use at most 128 MiB of HBM per device.

```python
import math
import jax
import jax.numpy as jnp
from jax import lax

Q_HEADS = 64
KV_HEADS = 8
HEAD = 128
BLOCK = 128
TREES = 8
TREE_BLOCKS = 16
TREE_LEN = 2048
Q_WIDTH = 8192
KV_WIDTH = 1024


def draw_query_input(key, part):
    return jnp.clip(jax.random.normal(jax.random.fold_in(key, 1), (TREES, TREE_LEN, Q_HEADS * HEAD), jnp.float32) * 1.4, -8.0, 8.0).astype(jnp.bfloat16)


def draw_key_input(key, part):
    return jnp.clip(jax.random.normal(jax.random.fold_in(key, 2), (TREES, TREE_LEN, KV_HEADS * HEAD), jnp.float32) * 1.4, -8.0, 8.0).astype(jnp.bfloat16)


def draw_parents(key, part):
    block_ids = jnp.broadcast_to(jnp.arange(TREE_BLOCKS, dtype=jnp.int32), (TREES, TREE_BLOCKS))
    coin_flips = jax.random.randint(jax.random.fold_in(key, 29), (TREES, TREE_BLOCKS), 0, 2)
    picked = jax.random.randint(jax.random.fold_in(key, 31), (TREES, TREE_BLOCKS), 0, jnp.maximum(block_ids, 1))
    chosen = jnp.where(coin_flips == 1, block_ids - 1, picked)
    chosen = jnp.where(block_ids == 0, 0, chosen)
    chosen = jnp.where(block_ids == TREE_BLOCKS - 1, TREE_BLOCKS - 2, chosen)
    return chosen.astype(jnp.int32)


def level_of(key, dims, pieces, smallest, largest):
    factor_of, own = 1.0, jax.random.fold_in(key, 6)
    for position, parts in pieces:
        steps = jnp.exp(jax.random.uniform(jax.random.fold_in(own, position), (parts,), jnp.float32, smallest / len(pieces), largest / len(pieces)))
        factor_of = factor_of * jnp.repeat(steps, dims[position] // parts).reshape([-1 if axis == position else 1 for axis in range(len(dims))])
    return factor_of


def gaussian(key, dims, deviation, most, split=(), kind=jnp.bfloat16):
    values = deviation * jax.random.normal(key, dims, jnp.float32)
    if split:
        values = values * level_of(key, dims, split, -0.22, 0.18)
    return jnp.clip(values, -most, most).astype(kind)


def setup_inputs(seed: int = 0) -> dict:
    streams_of = jax.random.split(jax.random.key(seed), 9)
    query_input = draw_query_input(jax.random.fold_in(streams_of[8], 71), 0)
    key_input = draw_key_input(jax.random.fold_in(streams_of[8], 71), 0)
    value_input = gaussian(streams_of[2], (TREES, TREE_LEN, KV_WIDTH), 1.0, 6.0, ((0, 8), (1, 16)))
    out_grad = gaussian(streams_of[3], (TREES, TREE_LEN, Q_WIDTH), 1.0, 6.0, ((0, 8), (1, 16)))
    query_bias = gaussian(streams_of[4], (Q_WIDTH,), 0.3, 1.75, (), jnp.float32)
    key_bias = gaussian(streams_of[5], (KV_WIDTH,), 0.3, 1.75, (), jnp.float32)
    value_bias = gaussian(streams_of[6], (KV_WIDTH,), 0.3, 1.75, (), jnp.float32)
    parents = draw_parents(jax.random.fold_in(streams_of[8], 71), 0)
    return {"query_input": query_input, "key_input": key_input, "value_input": value_input, "out_grad": out_grad, "query_bias": query_bias, "key_bias": key_bias, "value_bias": value_bias, "parents": parents}


LOG_BASE = math.log(1000000.0)
NEG_LARGE = -1e30


def ancestry(parent_list):
    block_count = parent_list.shape[0]
    block_ids = jnp.arange(block_count, dtype=jnp.int32)
    step_matrix = ((parent_list[:, None] == block_ids[None, :]) & (block_ids[:, None] > 0)).astype(jnp.float32)
    identity = jnp.eye(block_count, dtype=jnp.float32)

    def advance(iteration, current):
        return identity + jnp.dot(step_matrix, current, precision=lax.Precision.HIGHEST)

    return lax.fori_loop(0, block_count, advance, identity)


def rotate(values, places, direction):
    half_width = values.shape[-1] // 2
    frequency = jnp.exp(jnp.arange(half_width, dtype=jnp.float32) * (-2.0 * LOG_BASE / values.shape[-1]))
    angles = places[..., None] * frequency
    cosine = jnp.cos(angles)[..., None, :]
    sine_part = direction * jnp.sin(angles)[..., None, :]
    first_half = values[..., :half_width]
    second = values[..., half_width:]
    return jnp.concatenate([first_half * cosine - second * sine_part, second * cosine + first_half * sine_part], axis=-1)


def rounded(values):
    return lax.optimization_barrier(values.astype(jnp.bfloat16)).astype(jnp.float32)


def reference(query_input, key_input, value_input, out_grad, query_bias, key_bias, value_bias, parents):
    score_scale = HEAD ** -0.5
    group_size = Q_HEADS // KV_HEADS

    def one_tree(tree_items):
        query_tree, key_tree, value_tree, grad_tree, parent_list = tree_items
        ancestors = ancestry(parent_list)
        block_depth = jnp.sum(ancestors, axis=1) - 1.0
        offsets = jnp.arange(BLOCK, dtype=jnp.float32)
        places = (block_depth[:, None] * BLOCK + offsets[None, :]).reshape(TREE_LEN)
        queries = rotate((query_tree.astype(jnp.float32) + query_bias).reshape(TREE_LEN, Q_HEADS, HEAD), places, 1.0).astype(jnp.bfloat16)
        key_rows = rotate((key_tree.astype(jnp.float32) + key_bias).reshape(TREE_LEN, KV_HEADS, HEAD), places, 1.0).astype(jnp.bfloat16)
        value_rows = (value_tree.astype(jnp.float32) + value_bias).astype(jnp.bfloat16).reshape(TREE_LEN, KV_HEADS, HEAD)
        queries = queries.reshape(TREE_LEN, KV_HEADS, group_size, HEAD)
        grad_rows = grad_tree.reshape(TREE_LEN, KV_HEADS, group_size, HEAD)
        key_float = key_rows.astype(jnp.float32)
        value_float = value_rows.astype(jnp.float32)
        token_block = jnp.arange(TREE_LEN, dtype=jnp.int32) // BLOCK
        token_offset = jnp.arange(TREE_LEN, dtype=jnp.int32) % BLOCK
        row_offset = jnp.arange(BLOCK, dtype=jnp.int32)

        def per_block(carried, query_block):
            key_acc, value_acc, query_total = carried
            first_row = query_block * BLOCK
            query_tile = lax.dynamic_slice_in_dim(queries, first_row, BLOCK, 0).astype(jnp.float32)
            grad_tile = lax.dynamic_slice_in_dim(grad_rows, first_row, BLOCK, 0).astype(jnp.float32)
            reach_row = lax.dynamic_index_in_dim(ancestors, query_block, 0, keepdims=False)[token_block] > 0.5
            causal = (token_block[None, :] != query_block) | (token_offset[None, :] <= row_offset[:, None])
            tile_mask = (reach_row[None, :] & causal)[:, None, None, :]
            scores = jnp.einsum('qghd,kgd->qghk', query_tile, key_float) * score_scale
            scores = jnp.where(tile_mask, scores, NEG_LARGE)
            row_peak = jnp.max(scores, axis=-1)
            weights = jnp.where(tile_mask, jnp.exp(scores - row_peak[..., None]), 0.0)
            total_sum = jnp.sum(weights, axis=-1)
            mixed_sum = jnp.einsum('qghk,kgd->qghd', rounded(weights), value_float)
            out_tile = (mixed_sum / total_sum[..., None]).astype(jnp.bfloat16)
            log_total = row_peak + jnp.log(total_sum)
            row_delta = jnp.sum(grad_tile * out_tile.astype(jnp.float32), axis=-1)
            probabilities = jnp.where(tile_mask, jnp.exp(scores - log_total[..., None]), 0.0)
            grad_probs = jnp.einsum('qghd,kgd->qghk', grad_tile, value_float)
            grad_scores = probabilities * (grad_probs - row_delta[..., None])
            grad_low = rounded(grad_scores)
            query_rot = jnp.einsum('qghk,kgd->qghd', grad_low, key_float) * score_scale
            key_acc = key_acc + jnp.einsum('qghk,qghd->kgd', grad_low, query_tile) * score_scale
            value_acc = value_acc + jnp.einsum('qghk,qghd->kgd', rounded(probabilities), grad_tile)
            row_places = lax.dynamic_slice_in_dim(places, first_row, BLOCK, 0)
            query_full = rotate(query_rot.reshape(BLOCK, Q_HEADS, HEAD), row_places, -1.0).reshape(BLOCK, Q_WIDTH)
            return (key_acc, value_acc, query_total + jnp.sum(query_full, axis=0)), (out_tile.reshape(BLOCK, Q_WIDTH), query_full)

        start_carry = (jnp.zeros((TREE_LEN, KV_HEADS, HEAD), jnp.float32), jnp.zeros((TREE_LEN, KV_HEADS, HEAD), jnp.float32), jnp.zeros((Q_WIDTH,), jnp.float32))
        (key_acc, value_acc, query_total), (out_rows, query_rows) = lax.scan(per_block, start_carry, jnp.arange(TREE_BLOCKS, dtype=jnp.int32))
        key_full = rotate(key_acc, places, -1.0).reshape(TREE_LEN, KV_WIDTH)
        value_full = value_acc.reshape(TREE_LEN, KV_WIDTH)
        return (out_rows.reshape(TREE_LEN, Q_WIDTH), query_rows.reshape(TREE_LEN, Q_WIDTH), key_full, value_full, query_total, jnp.sum(key_full, axis=0), jnp.sum(value_full, axis=0))

    results = lax.map(one_tree, (query_input, key_input, value_input, out_grad, parents))
    return (results[0], results[1], results[2], results[3], jnp.sum(results[4], axis=0), jnp.sum(results[5], axis=0), jnp.sum(results[6], axis=0))
```

```python
import math

import jax
import jax.numpy as jnp
from jax import lax
from jax.sharding import PartitionSpec as P

Q_HEADS = 64
KV_HEADS = 8
HEAD = 128


LOG_BASE = math.log(1000000.0)
NEG_LARGE = -1e30


def ancestry(parent_list):
    block_count = parent_list.shape[0]
    block_ids = jnp.arange(block_count, dtype=jnp.int32)
    step_matrix = ((parent_list[:, None] == block_ids[None, :]) & (block_ids[:, None] > 0)).astype(
        jnp.float32
    )
    reach = jnp.eye(block_count, dtype=jnp.float32) + step_matrix
    steps = 1
    while steps < block_count:
        reach = jnp.minimum(jnp.dot(reach, reach, precision=lax.Precision.HIGHEST), 1.0)
        steps *= 2
    return reach


def rotate(values, places, direction):
    half_width = values.shape[-1] // 2
    frequency = jnp.exp(
        jnp.arange(half_width, dtype=jnp.float32) * (-2.0 * LOG_BASE / values.shape[-1])
    )
    angles = places[..., None] * frequency
    cosine = jnp.cos(angles)[..., None, :]
    sine_part = direction * jnp.sin(angles)[..., None, :]
    first_half = values[..., :half_width]
    second = values[..., half_width:]
    return jnp.concatenate(
        [first_half * cosine - second * sine_part, second * cosine + first_half * sine_part],
        axis=-1,
    )


def allowed_tiles(reach_values, same_block, row_count):
    row_ids = jnp.arange(row_count, dtype=jnp.int32)
    causal = row_ids[None, :] <= row_ids[:, None]
    return (reach_values[:, None, None] > 0.5) & (jnp.logical_not(same_block) | causal)[None]


def tile_forward(carried, query_tile, key_tile, value_tile, allowed, score_scale):
    running_max, running_sum, accumulated = carried
    tile_mask = allowed[:, :, None, None, :]
    scores = (
        jnp.einsum("tqghd,tkgd->tqghk", query_tile, key_tile, preferred_element_type=jnp.float32)
        * score_scale
    )
    scores = jnp.where(tile_mask, scores, NEG_LARGE)
    new_max = jnp.maximum(running_max, jnp.max(scores, axis=-1))
    weights = jnp.where(tile_mask, jnp.exp(scores - new_max[..., None]), 0.0)
    factor = jnp.exp(running_max - new_max)
    new_sum = running_sum * factor + jnp.sum(weights, axis=-1)
    mixed_sum = jnp.einsum(
        "tqghk,tkgd->tqghd",
        weights.astype(jnp.bfloat16),
        value_tile,
        preferred_element_type=jnp.float32,
    )
    return (new_max, new_sum, accumulated * factor[..., None] + mixed_sum)


def tile_backward(
    query_tile, key_tile, value_tile, grad_tile, log_total, row_delta, allowed, score_scale
):
    tile_mask = allowed[:, :, None, None, :]
    scores = (
        jnp.einsum("tqghd,tkgd->tqghk", query_tile, key_tile, preferred_element_type=jnp.float32)
        * score_scale
    )
    scores = jnp.where(tile_mask, scores, NEG_LARGE)
    probabilities = jnp.where(tile_mask, jnp.exp(scores - log_total[..., None]), 0.0)
    grad_probs = jnp.einsum(
        "tqghd,tkgd->tqghk", grad_tile, value_tile, preferred_element_type=jnp.float32
    )
    grad_scores = probabilities * (grad_probs - row_delta[..., None])
    grad_low = grad_scores.astype(jnp.bfloat16)
    query_part = (
        jnp.einsum("tqghk,tkgd->tqghd", grad_low, key_tile, preferred_element_type=jnp.float32)
        * score_scale
    )
    key_part = (
        jnp.einsum("tqghk,tqghd->tkgd", grad_low, query_tile, preferred_element_type=jnp.float32)
        * score_scale
    )
    value_part = jnp.einsum(
        "tqghk,tqghd->tkgd",
        probabilities.astype(jnp.bfloat16),
        grad_tile,
        preferred_element_type=jnp.float32,
    )
    return (query_part, key_part, value_part)


def body(query_input, key_input, value_input, out_grad, query_bias, key_bias, value_bias, parents):
    tree_count, row_count, query_width = query_input.shape
    key_width = key_input.shape[2]
    score_scale = HEAD ** (-0.5)
    group_size = Q_HEADS // KV_HEADS
    devices = lax.axis_size("ctx")
    device_index = lax.axis_index("ctx")
    raw_pair = jnp.stack([key_input, value_input], axis=2)
    gathered = lax.all_gather(raw_pair, "ctx", axis=1, tiled=True)
    ancestors = jax.vmap(ancestry)(parents)
    block_depth = jnp.sum(ancestors, axis=2) - 1.0
    offsets = jnp.arange(row_count, dtype=jnp.float32)
    all_places = block_depth[:, :, None] * row_count + offsets[None, None, :]
    own_places = lax.dynamic_index_in_dim(all_places, device_index, 1, keepdims=False)
    own_reach = lax.dynamic_index_in_dim(ancestors, device_index, 1, keepdims=False)
    queries = rotate(
        (query_input.astype(jnp.float32) + query_bias).reshape(
            tree_count, row_count, Q_HEADS, HEAD
        ),
        own_places,
        1.0,
    ).astype(jnp.bfloat16)
    tree_length = row_count * devices
    flat_places = all_places.reshape(tree_count, tree_length)
    key_piece = rotate(
        (gathered[:, :, 0].astype(jnp.float32) + key_bias).reshape(
            tree_count, tree_length, KV_HEADS, HEAD
        ),
        flat_places,
        1.0,
    ).astype(jnp.bfloat16)
    value_piece = (
        (gathered[:, :, 1].astype(jnp.float32) + value_bias)
        .astype(jnp.bfloat16)
        .reshape(tree_count, tree_length, KV_HEADS, HEAD)
    )
    query_tiles = queries.reshape(tree_count, row_count, KV_HEADS, group_size, HEAD)
    grad_tiles = out_grad.reshape(tree_count, row_count, KV_HEADS, group_size, HEAD)
    start_state = (
        jnp.full((tree_count, row_count, KV_HEADS, group_size), NEG_LARGE, jnp.float32),
        jnp.zeros((tree_count, row_count, KV_HEADS, group_size), jnp.float32),
        jnp.zeros((tree_count, row_count, KV_HEADS, group_size, HEAD), jnp.float32),
    )

    def one_block(block_step, current):
        key_tile = lax.dynamic_slice_in_dim(key_piece, block_step * row_count, row_count, 1)
        value_tile = lax.dynamic_slice_in_dim(value_piece, block_step * row_count, row_count, 1)
        reach_values = own_reach[:, block_step]
        allowed = allowed_tiles(reach_values, block_step == device_index, row_count)

        def compute():
            return tile_forward(current, query_tiles, key_tile, value_tile, allowed, score_scale)

        return lax.cond(jnp.any(reach_values > 0.5), compute, lambda: current)

    running_max, running_sum, accumulated = lax.fori_loop(0, devices, one_block, start_state)
    out_tiles = (accumulated / running_sum[..., None]).astype(jnp.bfloat16)
    log_total = running_max + jnp.log(running_sum)
    row_delta = jnp.sum(grad_tiles.astype(jnp.float32) * out_tiles.astype(jnp.float32), axis=-1)

    def one_grad_block(query_sum, block_step):
        key_tile = lax.dynamic_slice_in_dim(key_piece, block_step * row_count, row_count, 1)
        value_tile = lax.dynamic_slice_in_dim(value_piece, block_step * row_count, row_count, 1)
        block_places = lax.dynamic_index_in_dim(all_places, block_step, 1, keepdims=False)
        reach_values = own_reach[:, block_step]
        allowed = allowed_tiles(reach_values, block_step == device_index, row_count)

        def compute():
            query_part, key_part, value_part = tile_backward(
                query_tiles,
                key_tile,
                value_tile,
                grad_tiles,
                log_total,
                row_delta,
                allowed,
                score_scale,
            )
            key_back = rotate(key_part, block_places, -1.0)
            return (query_sum + query_part, key_back, value_part)

        def skip():
            zeros = jnp.zeros((tree_count, row_count, KV_HEADS, HEAD), jnp.float32)
            return (query_sum, zeros, zeros)

        new_sum, key_back, value_part = lax.cond(jnp.any(reach_values > 0.5), compute, skip)
        return new_sum, (key_back, value_part)

    query_sum, (key_parts, value_parts) = lax.scan(
        one_grad_block,
        jnp.zeros((tree_count, row_count, KV_HEADS, group_size, HEAD), jnp.float32),
        jnp.arange(devices, dtype=jnp.int32),
    )
    key_total = jnp.sum(key_parts, axis=(0, 1, 2)).reshape(key_width)
    value_total = jnp.sum(value_parts, axis=(0, 1, 2)).reshape(key_width)
    stacked = jnp.stack(
        [
            key_parts.reshape(devices, tree_count, row_count, key_width),
            value_parts.reshape(devices, tree_count, row_count, key_width),
        ],
        axis=3,
    ).astype(jnp.bfloat16)
    own_grads = lax.psum_scatter(stacked, "ctx", scatter_dimension=0, tiled=True)[0].astype(
        jnp.float32
    )
    key_full = own_grads[:, :, 0]
    value_full = own_grads[:, :, 1]
    query_full = rotate(
        query_sum.reshape(tree_count, row_count, Q_HEADS, HEAD), own_places, -1.0
    ).reshape(tree_count, row_count, query_width)
    attended = out_tiles.reshape(tree_count, row_count, query_width)
    query_total = jnp.sum(query_full, axis=(0, 1))
    query_total, key_total, value_total = lax.psum(
        (query_total, key_total, value_total), ("dp", "ctx")
    )
    return (attended, query_full, key_full, value_full, query_total, key_total, value_total)


def solution(mesh):
    placed = (
        P("dp", "ctx", None),
        P("dp", "ctx", None),
        P("dp", "ctx", None),
        P("dp", "ctx", None),
        P(),
        P(),
        P(),
        P("dp", None),
    )
    return jax.shard_map(
        body,
        mesh=mesh,
        in_specs=placed,
        out_specs=(
            P("dp", "ctx", None),
            P("dp", "ctx", None),
            P("dp", "ctx", None),
            P("dp", "ctx", None),
            P(),
            P(),
            P(),
        ),
        check_vma=False,
    )
```

```python
import math

import jax
import jax.numpy as jnp
from jax import lax
from jax.sharding import PartitionSpec as P

Q_HEADS = 64
KV_HEADS = 8
HEAD = 128


LOG_BASE = math.log(1000000.0)
NEG_LARGE = -1e30


def ancestry(parent_list):
    block_count = parent_list.shape[0]
    block_ids = jnp.arange(block_count, dtype=jnp.int32)
    step_matrix = ((parent_list[:, None] == block_ids[None, :]) & (block_ids[:, None] > 0)).astype(
        jnp.float32
    )
    reach = jnp.eye(block_count, dtype=jnp.float32) + step_matrix
    steps = 1
    while steps < block_count:
        reach = jnp.minimum(jnp.dot(reach, reach, precision=lax.Precision.HIGHEST), 1.0)
        steps *= 2
    return reach


def rotate(values, places, direction):
    half_width = values.shape[-1] // 2
    frequency = jnp.exp(
        jnp.arange(half_width, dtype=jnp.float32) * (-2.0 * LOG_BASE / values.shape[-1])
    )
    angles = places[..., None] * frequency
    cosine = jnp.cos(angles)[..., None, :]
    sine_part = direction * jnp.sin(angles)[..., None, :]
    first_half = values[..., :half_width]
    second = values[..., half_width:]
    return jnp.concatenate(
        [first_half * cosine - second * sine_part, second * cosine + first_half * sine_part],
        axis=-1,
    )


def allowed_tiles(reach_values, same_block, row_count):
    row_ids = jnp.arange(row_count, dtype=jnp.int32)
    causal = row_ids[None, :] <= row_ids[:, None]
    return (reach_values[:, None, None] > 0.5) & (jnp.logical_not(same_block) | causal)[None]


def tile_forward(carried, query_tile, key_tile, value_tile, allowed, score_scale):
    running_max, running_sum, accumulated = carried
    tile_mask = allowed[:, :, None, None, :]
    scores = (
        jnp.einsum("tqghd,tkgd->tqghk", query_tile, key_tile, preferred_element_type=jnp.float32)
        * score_scale
    )
    scores = jnp.where(tile_mask, scores, NEG_LARGE)
    new_max = jnp.maximum(running_max, jnp.max(scores, axis=-1))
    weights = jnp.where(tile_mask, jnp.exp(scores - new_max[..., None]), 0.0)
    factor = jnp.exp(running_max - new_max)
    new_sum = running_sum * factor + jnp.sum(weights, axis=-1)
    mixed_sum = jnp.einsum(
        "tqghk,tkgd->tqghd",
        weights.astype(jnp.bfloat16),
        value_tile,
        preferred_element_type=jnp.float32,
    )
    return (new_max, new_sum, accumulated * factor[..., None] + mixed_sum)


def tile_backward(
    query_tile, key_tile, value_tile, grad_tile, log_total, row_delta, allowed, score_scale
):
    tile_mask = allowed[:, :, None, None, :]
    scores = (
        jnp.einsum("tqghd,tkgd->tqghk", query_tile, key_tile, preferred_element_type=jnp.float32)
        * score_scale
    )
    scores = jnp.where(tile_mask, scores, NEG_LARGE)
    probabilities = jnp.where(tile_mask, jnp.exp(scores - log_total[..., None]), 0.0)
    grad_probs = jnp.einsum(
        "tqghd,tkgd->tqghk", grad_tile, value_tile, preferred_element_type=jnp.float32
    )
    grad_scores = probabilities * (grad_probs - row_delta[..., None])
    grad_low = grad_scores.astype(jnp.bfloat16)
    query_part = (
        jnp.einsum("tqghk,tkgd->tqghd", grad_low, key_tile, preferred_element_type=jnp.float32)
        * score_scale
    )
    key_part = (
        jnp.einsum("tqghk,tqghd->tkgd", grad_low, query_tile, preferred_element_type=jnp.float32)
        * score_scale
    )
    value_part = jnp.einsum(
        "tqghk,tqghd->tkgd",
        probabilities.astype(jnp.bfloat16),
        grad_tile,
        preferred_element_type=jnp.float32,
    )
    return (query_part, key_part, value_part)


def body(query_input, key_input, value_input, out_grad, query_bias, key_bias, value_bias, parents):
    tree_count, row_count, query_width = query_input.shape
    key_width = key_input.shape[2]
    score_scale = HEAD ** (-0.5)
    group_size = Q_HEADS // KV_HEADS
    devices = lax.axis_size("ctx")
    device_index = lax.axis_index("ctx")
    raw_pair = jnp.stack([key_input, value_input], axis=2)
    received = [raw_pair]
    for shift in range(1, devices):
        pairs = [(i, i + shift) for i in range(devices - shift)]
        received.append(lax.ppermute(raw_pair, "ctx", pairs))
    ancestors = jax.vmap(ancestry)(parents)
    block_depth = jnp.sum(ancestors, axis=2) - 1.0
    offsets = jnp.arange(row_count, dtype=jnp.float32)
    all_places = block_depth[:, :, None] * row_count + offsets[None, None, :]
    own_places = lax.dynamic_index_in_dim(all_places, device_index, 1, keepdims=False)
    own_reach = lax.dynamic_index_in_dim(ancestors, device_index, 1, keepdims=False)
    shift_ids = jnp.arange(devices, dtype=jnp.int32)
    shift_blocks = device_index - shift_ids
    shift_valid = shift_blocks >= 0
    safe_blocks = jnp.maximum(shift_blocks, 0)
    shift_reach = jnp.where(shift_valid[:, None], jnp.take(own_reach, safe_blocks, axis=1).T, 0.0)
    shift_places = jnp.transpose(jnp.take(all_places, safe_blocks, axis=1), (1, 0, 2))
    queries = rotate(
        (query_input.astype(jnp.float32) + query_bias).reshape(
            tree_count, row_count, Q_HEADS, HEAD
        ),
        own_places,
        1.0,
    ).astype(jnp.bfloat16)
    kv_stack = jnp.stack(received, axis=0)
    key_stack = rotate(
        (kv_stack[:, :, :, 0].astype(jnp.float32) + key_bias).reshape(
            devices, tree_count, row_count, KV_HEADS, HEAD
        ),
        shift_places,
        1.0,
    ).astype(jnp.bfloat16)
    value_stack = (
        (kv_stack[:, :, :, 1].astype(jnp.float32) + value_bias)
        .astype(jnp.bfloat16)
        .reshape(devices, tree_count, row_count, KV_HEADS, HEAD)
    )
    query_tiles = queries.reshape(tree_count, row_count, KV_HEADS, group_size, HEAD)
    grad_tiles = out_grad.reshape(tree_count, row_count, KV_HEADS, group_size, HEAD)
    start_state = (
        jnp.full((tree_count, row_count, KV_HEADS, group_size), NEG_LARGE, jnp.float32),
        jnp.zeros((tree_count, row_count, KV_HEADS, group_size), jnp.float32),
        jnp.zeros((tree_count, row_count, KV_HEADS, group_size, HEAD), jnp.float32),
    )

    def one_block(shift, current):
        key_tile = key_stack[shift]
        value_tile = value_stack[shift]
        reach_values = shift_reach[shift]
        allowed = allowed_tiles(reach_values, shift == 0, row_count)

        def compute():
            return tile_forward(current, query_tiles, key_tile, value_tile, allowed, score_scale)

        return lax.cond(jnp.any(reach_values > 0.5), compute, lambda: current)

    running_max, running_sum, accumulated = lax.fori_loop(0, devices, one_block, start_state)
    out_tiles = (accumulated / running_sum[..., None]).astype(jnp.bfloat16)
    log_total = running_max + jnp.log(running_sum)
    row_delta = jnp.sum(grad_tiles.astype(jnp.float32) * out_tiles.astype(jnp.float32), axis=-1)

    def one_grad_block(query_sum, shift):
        key_tile = key_stack[shift]
        value_tile = value_stack[shift]
        reach_values = shift_reach[shift]
        allowed = allowed_tiles(reach_values, shift == 0, row_count)

        def compute():
            query_part, key_part, value_part = tile_backward(
                query_tiles,
                key_tile,
                value_tile,
                grad_tiles,
                log_total,
                row_delta,
                allowed,
                score_scale,
            )
            return (query_sum + query_part, key_part, value_part)

        def skip():
            zeros = jnp.zeros((tree_count, row_count, KV_HEADS, HEAD), jnp.float32)
            return (query_sum, zeros, zeros)

        new_sum, key_part, value_part = lax.cond(jnp.any(reach_values > 0.5), compute, skip)
        return new_sum, (key_part, value_part)

    query_sum, (key_parts, value_parts) = lax.scan(
        one_grad_block,
        jnp.zeros((tree_count, row_count, KV_HEADS, group_size, HEAD), jnp.float32),
        shift_ids,
    )
    key_parts = rotate(key_parts, shift_places, -1.0)
    key_total = jnp.sum(key_parts, axis=(0, 1, 2)).reshape(key_width)
    value_total = jnp.sum(value_parts, axis=(0, 1, 2)).reshape(key_width)
    grad_stack = jnp.stack(
        [
            key_parts.reshape(devices, tree_count, row_count, key_width),
            value_parts.reshape(devices, tree_count, row_count, key_width),
        ],
        axis=3,
    )
    own_grads = grad_stack[0]
    for shift in range(1, devices):
        pairs = [(i, i - shift) for i in range(shift, devices)]
        arrived = lax.ppermute(grad_stack[shift].astype(jnp.bfloat16), "ctx", pairs)
        own_grads = own_grads + arrived.astype(jnp.float32)
    key_full = own_grads[:, :, 0]
    value_full = own_grads[:, :, 1]
    query_full = rotate(
        query_sum.reshape(tree_count, row_count, Q_HEADS, HEAD), own_places, -1.0
    ).reshape(tree_count, row_count, query_width)
    attended = out_tiles.reshape(tree_count, row_count, query_width)
    query_total = jnp.sum(query_full, axis=(0, 1))
    query_total, key_total, value_total = lax.psum(
        (query_total, key_total, value_total), ("dp", "ctx")
    )
    return (attended, query_full, key_full, value_full, query_total, key_total, value_total)


def solution(mesh):
    placed = (
        P("dp", "ctx", None),
        P("dp", "ctx", None),
        P("dp", "ctx", None),
        P("dp", "ctx", None),
        P(),
        P(),
        P(),
        P("dp", None),
    )
    return jax.shard_map(
        body,
        mesh=mesh,
        in_specs=placed,
        out_specs=(
            P("dp", "ctx", None),
            P("dp", "ctx", None),
            P("dp", "ctx", None),
            P("dp", "ctx", None),
            P(),
            P(),
            P(),
        ),
        check_vma=False,
    )
```

```python
import functools
import math

import jax
import jax.numpy as jnp
from jax import lax
from jax.experimental import pallas as pl
from jax.experimental.pallas import tpu as pltpu
from jax.sharding import PartitionSpec as P

Q_HEADS = 64
KV_HEADS = 8
HEAD = 128


LOG_BASE = math.log(1000000.0)
NEG_LARGE = -1e30


def ancestry(parent_list):
    block_count = parent_list.shape[0]
    block_ids = jnp.arange(block_count, dtype=jnp.int32)
    step_matrix = ((parent_list[:, None] == block_ids[None, :]) & (block_ids[:, None] > 0)).astype(
        jnp.float32
    )
    reach = jnp.eye(block_count, dtype=jnp.float32) + step_matrix
    steps = 1
    while steps < block_count:
        reach = jnp.minimum(jnp.dot(reach, reach, precision=lax.Precision.HIGHEST), 1.0)
        steps *= 2
    return reach


def rotate(values, places, direction):
    half_width = values.shape[-1] // 2
    frequency = jnp.exp(
        jnp.arange(half_width, dtype=jnp.float32) * (-2.0 * LOG_BASE / values.shape[-1])
    )
    angles = places[..., None] * frequency
    cosine = jnp.cos(angles)[..., None, :]
    sine_part = direction * jnp.sin(angles)[..., None, :]
    first_half = values[..., :half_width]
    second = values[..., half_width:]
    return jnp.concatenate(
        [first_half * cosine - second * sine_part, second * cosine + first_half * sine_part],
        axis=-1,
    )


def allowed_tiles(reach_values, same_block, row_count):
    row_ids = jnp.arange(row_count, dtype=jnp.int32)
    causal = row_ids[None, :] <= row_ids[:, None]
    return (reach_values[:, None, None] > 0.5) & (jnp.logical_not(same_block) | causal)[None]


def _visible(block, own, rows):
    row_ids = lax.broadcasted_iota(jnp.int32, (rows, rows), 0)
    col_ids = lax.broadcasted_iota(jnp.int32, (rows, rows), 1)
    return jnp.logical_or(block != own, col_ids <= row_ids)


def _fwd_kernel(reach_ref, own_ref, q_ref, k_ref, v_ref, o_ref, lse_ref, m_scr, l_scr, acc_scr,
                *, heads, head, scale):
    block = pl.program_id(1)
    last = pl.num_programs(1) - 1
    rows = q_ref.shape[0]

    @pl.when(block == 0)
    def _():
        m_scr[...] = jnp.full(m_scr.shape, NEG_LARGE, jnp.float32)
        l_scr[...] = jnp.zeros(l_scr.shape, jnp.float32)
        acc_scr[...] = jnp.zeros(acc_scr.shape, jnp.float32)

    @pl.when(reach_ref[block] > 0)
    def _():
        mask = _visible(block, own_ref[0], rows)
        key = k_ref[0]
        value = v_ref[0]
        for h in range(heads):
            query = q_ref[:, h * head:(h + 1) * head]
            scores = lax.dot_general(query, key, (((1,), (1,)), ((), ())),
                                     preferred_element_type=jnp.float32) * scale
            scores = jnp.where(mask, scores, NEG_LARGE)
            m_prev = m_scr[h]
            m_new = jnp.maximum(m_prev, jnp.max(scores, axis=-1, keepdims=True))
            weights = jnp.where(mask, jnp.exp(scores - m_new), 0.0)
            factor = jnp.exp(m_prev - m_new)
            l_scr[h] = l_scr[h] * factor + jnp.sum(weights, axis=-1, keepdims=True)
            mixed = jnp.dot(weights.astype(jnp.bfloat16), value, preferred_element_type=jnp.float32)
            acc_scr[h] = acc_scr[h] * factor + mixed
            m_scr[h] = m_new

    @pl.when(block == last)
    def _():
        for h in range(heads):
            total = l_scr[h]
            o_ref[:, h * head:(h + 1) * head] = (acc_scr[h] / total).astype(o_ref.dtype)
            lse_ref[h] = m_scr[h] + jnp.log(total)


def flash_forward(reach, own, queries, key_stack, value_stack, *, heads, head, scale, interpret=False):
    rows, width = queries.shape
    blocks = key_stack.shape[0]
    groups = width // (heads * head)
    kernel = functools.partial(_fwd_kernel, heads=heads, head=head, scale=scale)
    grid_spec = pltpu.PrefetchScalarGridSpec(
        num_scalar_prefetch=2,
        grid=(groups, blocks),
        in_specs=[
            pl.BlockSpec((rows, heads * head), lambda g, b, r, o: (0, g)),
            pl.BlockSpec((1, rows, head), lambda g, b, r, o: (b, 0, g)),
            pl.BlockSpec((1, rows, head), lambda g, b, r, o: (b, 0, g)),
        ],
        out_specs=[
            pl.BlockSpec((rows, heads * head), lambda g, b, r, o: (0, g)),
            pl.BlockSpec((heads, rows, 1), lambda g, b, r, o: (g, 0, 0)),
        ],
        scratch_shapes=[
            pltpu.VMEM((heads, rows, 1), jnp.float32),
            pltpu.VMEM((heads, rows, 1), jnp.float32),
            pltpu.VMEM((heads, rows, head), jnp.float32),
        ],
    )
    return pl.pallas_call(
        kernel,
        grid_spec=grid_spec,
        out_shape=[
            jax.ShapeDtypeStruct((rows, width), jnp.bfloat16),
            jax.ShapeDtypeStruct((groups * heads, rows, 1), jnp.float32),
        ],
        compiler_params=pltpu.CompilerParams(dimension_semantics=("arbitrary", "arbitrary")),
        interpret=interpret,
    )(reach, own, queries, key_stack, value_stack)


def _bwd_kernel(reach_ref, own_ref, q_ref, do_ref, k_ref, v_ref, lse_ref, delta_ref,
                dq_ref, dk_ref, dv_ref, dq_scr, *, heads, head, scale):
    block = pl.program_id(1)
    last = pl.num_programs(1) - 1
    rows = q_ref.shape[0]

    @pl.when(block == 0)
    def _():
        dq_scr[...] = jnp.zeros(dq_scr.shape, jnp.float32)

    @pl.when(reach_ref[block] > 0)
    def _():
        mask = _visible(block, own_ref[0], rows)
        key = k_ref[0]
        value = v_ref[0]
        key_acc = jnp.zeros((rows, head), jnp.float32)
        value_acc = jnp.zeros((rows, head), jnp.float32)
        for h in range(heads):
            query = q_ref[:, h * head:(h + 1) * head]
            grad = do_ref[:, h * head:(h + 1) * head]
            scores = lax.dot_general(query, key, (((1,), (1,)), ((), ())),
                                     preferred_element_type=jnp.float32) * scale
            scores = jnp.where(mask, scores, NEG_LARGE)
            probs = jnp.where(mask, jnp.exp(scores - lse_ref[h]), 0.0)
            grad_probs = lax.dot_general(grad, value, (((1,), (1,)), ((), ())),
                                         preferred_element_type=jnp.float32)
            grad_low = (probs * (grad_probs - delta_ref[h])).astype(jnp.bfloat16)
            dq_scr[h] = dq_scr[h] + jnp.dot(grad_low, key, preferred_element_type=jnp.float32) * scale
            key_acc = key_acc + lax.dot_general(grad_low, query, (((0,), (0,)), ((), ())),
                                                preferred_element_type=jnp.float32)
            value_acc = value_acc + lax.dot_general(probs.astype(jnp.bfloat16), grad,
                                                    (((0,), (0,)), ((), ())),
                                                    preferred_element_type=jnp.float32)
        dk_ref[0] = key_acc * scale
        dv_ref[0] = value_acc

    @pl.when(reach_ref[block] == 0)
    def _():
        dk_ref[...] = jnp.zeros(dk_ref.shape, jnp.float32)
        dv_ref[...] = jnp.zeros(dv_ref.shape, jnp.float32)

    @pl.when(block == last)
    def _():
        for h in range(heads):
            dq_ref[:, h * head:(h + 1) * head] = dq_scr[h]


def flash_backward(reach, own, queries, out_grad, key_stack, value_stack, lse, delta,
                   *, heads, head, scale, interpret=False):
    rows, width = queries.shape
    blocks = key_stack.shape[0]
    kv_width = key_stack.shape[2]
    groups = width // (heads * head)
    kernel = functools.partial(_bwd_kernel, heads=heads, head=head, scale=scale)
    grid_spec = pltpu.PrefetchScalarGridSpec(
        num_scalar_prefetch=2,
        grid=(groups, blocks),
        in_specs=[
            pl.BlockSpec((rows, heads * head), lambda g, b, r, o: (0, g)),
            pl.BlockSpec((rows, heads * head), lambda g, b, r, o: (0, g)),
            pl.BlockSpec((1, rows, head), lambda g, b, r, o: (b, 0, g)),
            pl.BlockSpec((1, rows, head), lambda g, b, r, o: (b, 0, g)),
            pl.BlockSpec((heads, rows, 1), lambda g, b, r, o: (g, 0, 0)),
            pl.BlockSpec((heads, rows, 1), lambda g, b, r, o: (g, 0, 0)),
        ],
        out_specs=[
            pl.BlockSpec((rows, heads * head), lambda g, b, r, o: (0, g)),
            pl.BlockSpec((1, rows, head), lambda g, b, r, o: (b, 0, g)),
            pl.BlockSpec((1, rows, head), lambda g, b, r, o: (b, 0, g)),
        ],
        scratch_shapes=[pltpu.VMEM((heads, rows, head), jnp.float32)],
    )
    return pl.pallas_call(
        kernel,
        grid_spec=grid_spec,
        out_shape=[
            jax.ShapeDtypeStruct((rows, width), jnp.float32),
            jax.ShapeDtypeStruct((blocks, rows, kv_width), jnp.float32),
            jax.ShapeDtypeStruct((blocks, rows, kv_width), jnp.float32),
        ],
        compiler_params=pltpu.CompilerParams(dimension_semantics=("arbitrary", "arbitrary")),
        interpret=interpret,
    )(reach, own, queries, out_grad, key_stack, value_stack, lse, delta)


def body(query_input, key_input, value_input, out_grad, query_bias, key_bias, value_bias, parents):
    tree_count, row_count, query_width = query_input.shape
    key_width = key_input.shape[2]
    score_scale = HEAD ** (-0.5)
    group_size = Q_HEADS // KV_HEADS
    devices = lax.axis_size("ctx")
    device_index = lax.axis_index("ctx")
    raw_pair = jnp.stack([key_input, value_input], axis=2)
    gathered = lax.all_gather(raw_pair, "ctx", axis=1, tiled=True)
    ancestors = jax.vmap(ancestry)(parents)
    block_depth = jnp.sum(ancestors, axis=2) - 1.0
    offsets = jnp.arange(row_count, dtype=jnp.float32)
    all_places = block_depth[:, :, None] * row_count + offsets[None, None, :]
    own_places = lax.dynamic_index_in_dim(all_places, device_index, 1, keepdims=False)
    own_reach = lax.dynamic_index_in_dim(ancestors, device_index, 1, keepdims=False)
    queries = rotate(
        (query_input.astype(jnp.float32) + query_bias).reshape(
            tree_count, row_count, Q_HEADS, HEAD
        ),
        own_places,
        1.0,
    ).astype(jnp.bfloat16)
    tree_length = row_count * devices
    flat_places = all_places.reshape(tree_count, tree_length)
    key_piece = rotate(
        (gathered[:, :, 0].astype(jnp.float32) + key_bias).reshape(
            tree_count, tree_length, KV_HEADS, HEAD
        ),
        flat_places,
        1.0,
    ).astype(jnp.bfloat16)
    value_piece = (
        (gathered[:, :, 1].astype(jnp.float32) + value_bias)
        .astype(jnp.bfloat16)
        .reshape(tree_count, tree_length, KV_HEADS, HEAD)
    )
    reach_flags = (own_reach[0] > 0.5).astype(jnp.int32)
    own_block = jnp.reshape(device_index, (1,)).astype(jnp.int32)
    flat_queries = queries.reshape(row_count, query_width)
    flat_grads = out_grad.reshape(row_count, query_width)
    key_stack = key_piece.reshape(devices, row_count, key_width)
    value_stack = value_piece.reshape(devices, row_count, key_width)
    out_rows, log_total = flash_forward(
        reach_flags, own_block, flat_queries, key_stack, value_stack,
        heads=group_size, head=HEAD, scale=score_scale,
    )
    row_delta = jnp.sum(
        (flat_grads.astype(jnp.float32) * out_rows.astype(jnp.float32)).reshape(
            row_count, Q_HEADS, HEAD
        ),
        axis=-1,
    )
    row_delta = jnp.transpose(row_delta, (1, 0))[:, :, None]
    query_sum, key_parts, value_parts = flash_backward(
        reach_flags, own_block, flat_queries, flat_grads, key_stack, value_stack,
        log_total, row_delta, heads=group_size, head=HEAD, scale=score_scale,
    )
    key_parts = rotate(
        key_parts.reshape(devices, row_count, KV_HEADS, HEAD), all_places[0], -1.0
    ).reshape(devices, row_count, key_width)
    key_total = jnp.sum(key_parts, axis=(0, 1))
    value_total = jnp.sum(value_parts, axis=(0, 1))
    stacked = jnp.stack([key_parts, value_parts], axis=2).astype(jnp.bfloat16)
    stacked = stacked.reshape(devices, tree_count, row_count, 2, key_width)
    arrived = lax.all_to_all(stacked, "ctx", 0, 0, tiled=True)
    own_grads = jnp.sum(arrived.astype(jnp.float32), axis=0)
    key_full = own_grads[:, :, 0]
    value_full = own_grads[:, :, 1]
    query_full = rotate(
        query_sum.reshape(tree_count, row_count, Q_HEADS, HEAD), own_places, -1.0
    ).reshape(tree_count, row_count, query_width)
    attended = out_rows.reshape(tree_count, row_count, query_width)
    query_total = jnp.sum(query_full, axis=(0, 1))
    query_total, key_total, value_total = lax.psum(
        (query_total, key_total, value_total), ("dp", "ctx")
    )
    return (attended, query_full, key_full, value_full, query_total, key_total, value_total)


def solution(mesh):
    placed = (
        P("dp", "ctx", None),
        P("dp", "ctx", None),
        P("dp", "ctx", None),
        P("dp", "ctx", None),
        P(),
        P(),
        P(),
        P("dp", None),
    )
    return jax.shard_map(
        body,
        mesh=mesh,
        in_specs=placed,
        out_specs=(
            P("dp", "ctx", None),
            P("dp", "ctx", None),
            P("dp", "ctx", None),
            P("dp", "ctx", None),
            P(),
            P(),
            P(),
        ),
        check_vma=False,
    )
```

```python
import functools
import math

import jax
import jax.numpy as jnp
from jax import lax
from jax.experimental import pallas as pl
from jax.experimental.pallas import tpu as pltpu
from jax.sharding import PartitionSpec as P

Q_HEADS = 64
KV_HEADS = 8
HEAD = 128


LOG_BASE = math.log(1000000.0)
NEG_LARGE = -1e30


def ancestry(parent_list):
    block_count = parent_list.shape[0]
    block_ids = jnp.arange(block_count, dtype=jnp.int32)
    step_matrix = ((parent_list[:, None] == block_ids[None, :]) & (block_ids[:, None] > 0)).astype(
        jnp.float32
    )
    reach = jnp.eye(block_count, dtype=jnp.float32) + step_matrix
    steps = 1
    while steps < block_count:
        reach = jnp.minimum(jnp.dot(reach, reach, precision=lax.Precision.HIGHEST), 1.0)
        steps *= 2
    return reach


def rotate(values, places, direction):
    half_width = values.shape[-1] // 2
    frequency = jnp.exp(
        jnp.arange(half_width, dtype=jnp.float32) * (-2.0 * LOG_BASE / values.shape[-1])
    )
    angles = places[..., None] * frequency
    cosine = jnp.cos(angles)[..., None, :]
    sine_part = direction * jnp.sin(angles)[..., None, :]
    first_half = values[..., :half_width]
    second = values[..., half_width:]
    return jnp.concatenate(
        [first_half * cosine - second * sine_part, second * cosine + first_half * sine_part],
        axis=-1,
    )


def allowed_tiles(reach_values, same_block, row_count):
    row_ids = jnp.arange(row_count, dtype=jnp.int32)
    causal = row_ids[None, :] <= row_ids[:, None]
    return (reach_values[:, None, None] > 0.5) & (jnp.logical_not(same_block) | causal)[None]


def _visible(block, own, rows):
    row_ids = lax.broadcasted_iota(jnp.int32, (rows, rows), 0)
    col_ids = lax.broadcasted_iota(jnp.int32, (rows, rows), 1)
    return jnp.logical_or(block != own, col_ids <= row_ids)


def _fwd_kernel(reach_ref, own_ref, q_ref, k_ref, v_ref, o_ref, lse_ref, m_scr, l_scr, acc_scr,
                *, heads, head, scale):
    block = pl.program_id(1)
    last = pl.num_programs(1) - 1
    rows = q_ref.shape[0]

    @pl.when(block == 0)
    def _():
        m_scr[...] = jnp.full(m_scr.shape, NEG_LARGE, jnp.float32)
        l_scr[...] = jnp.zeros(l_scr.shape, jnp.float32)
        acc_scr[...] = jnp.zeros(acc_scr.shape, jnp.float32)

    @pl.when(reach_ref[block] > 0)
    def _():
        mask = _visible(block, own_ref[0], rows)
        key = k_ref[0]
        value = v_ref[0]
        for h in range(heads):
            query = q_ref[:, h * head:(h + 1) * head]
            scores = lax.dot_general(query, key, (((1,), (1,)), ((), ())),
                                     preferred_element_type=jnp.float32) * scale
            scores = jnp.where(mask, scores, NEG_LARGE)
            m_prev = m_scr[h]
            m_new = jnp.maximum(m_prev, jnp.max(scores, axis=-1, keepdims=True))
            weights = jnp.where(mask, jnp.exp(scores - m_new), 0.0)
            factor = jnp.exp(m_prev - m_new)
            l_scr[h] = l_scr[h] * factor + jnp.sum(weights, axis=-1, keepdims=True)
            mixed = jnp.dot(weights.astype(jnp.bfloat16), value, preferred_element_type=jnp.float32)
            acc_scr[h] = acc_scr[h] * factor + mixed
            m_scr[h] = m_new

    @pl.when(block == last)
    def _():
        for h in range(heads):
            total = l_scr[h]
            o_ref[:, h * head:(h + 1) * head] = (acc_scr[h] / total).astype(o_ref.dtype)
            lse_ref[h] = m_scr[h] + jnp.log(total)


def flash_forward(reach, own, queries, key_stack, value_stack, *, heads, head, scale, interpret=False):
    rows, width = queries.shape
    blocks = key_stack.shape[0]
    groups = width // (heads * head)
    kernel = functools.partial(_fwd_kernel, heads=heads, head=head, scale=scale)
    grid_spec = pltpu.PrefetchScalarGridSpec(
        num_scalar_prefetch=2,
        grid=(groups, blocks),
        in_specs=[
            pl.BlockSpec((rows, heads * head), lambda g, b, r, o: (0, g)),
            pl.BlockSpec((1, rows, head), lambda g, b, r, o: (b, 0, g)),
            pl.BlockSpec((1, rows, head), lambda g, b, r, o: (b, 0, g)),
        ],
        out_specs=[
            pl.BlockSpec((rows, heads * head), lambda g, b, r, o: (0, g)),
            pl.BlockSpec((heads, rows, 1), lambda g, b, r, o: (g, 0, 0)),
        ],
        scratch_shapes=[
            pltpu.VMEM((heads, rows, 1), jnp.float32),
            pltpu.VMEM((heads, rows, 1), jnp.float32),
            pltpu.VMEM((heads, rows, head), jnp.float32),
        ],
    )
    return pl.pallas_call(
        kernel,
        grid_spec=grid_spec,
        out_shape=[
            jax.ShapeDtypeStruct((rows, width), jnp.bfloat16),
            jax.ShapeDtypeStruct((groups * heads, rows, 1), jnp.float32),
        ],
        compiler_params=pltpu.CompilerParams(dimension_semantics=("arbitrary", "arbitrary")),
        interpret=interpret,
    )(reach, own, queries, key_stack, value_stack)


def _bwd_kernel(reach_ref, own_ref, q_ref, do_ref, k_ref, v_ref, lse_ref, delta_ref,
                dq_ref, dk_ref, dv_ref, dq_scr, *, heads, head, scale):
    block = pl.program_id(1)
    last = pl.num_programs(1) - 1
    rows = q_ref.shape[0]

    @pl.when(block == 0)
    def _():
        dq_scr[...] = jnp.zeros(dq_scr.shape, jnp.float32)

    @pl.when(reach_ref[block] > 0)
    def _():
        mask = _visible(block, own_ref[0], rows)
        key = k_ref[0]
        value = v_ref[0]
        key_acc = jnp.zeros((rows, head), jnp.float32)
        value_acc = jnp.zeros((rows, head), jnp.float32)
        for h in range(heads):
            query = q_ref[:, h * head:(h + 1) * head]
            grad = do_ref[:, h * head:(h + 1) * head]
            scores = lax.dot_general(query, key, (((1,), (1,)), ((), ())),
                                     preferred_element_type=jnp.float32) * scale
            scores = jnp.where(mask, scores, NEG_LARGE)
            probs = jnp.where(mask, jnp.exp(scores - lse_ref[h]), 0.0)
            grad_probs = lax.dot_general(grad, value, (((1,), (1,)), ((), ())),
                                         preferred_element_type=jnp.float32)
            grad_low = (probs * (grad_probs - delta_ref[h])).astype(jnp.bfloat16)
            dq_scr[h] = dq_scr[h] + jnp.dot(grad_low, key, preferred_element_type=jnp.float32) * scale
            key_acc = key_acc + lax.dot_general(grad_low, query, (((0,), (0,)), ((), ())),
                                                preferred_element_type=jnp.float32)
            value_acc = value_acc + lax.dot_general(probs.astype(jnp.bfloat16), grad,
                                                    (((0,), (0,)), ((), ())),
                                                    preferred_element_type=jnp.float32)
        dk_ref[0] = key_acc * scale
        dv_ref[0] = value_acc

    @pl.when(reach_ref[block] == 0)
    def _():
        dk_ref[...] = jnp.zeros(dk_ref.shape, jnp.float32)
        dv_ref[...] = jnp.zeros(dv_ref.shape, jnp.float32)

    @pl.when(block == last)
    def _():
        for h in range(heads):
            dq_ref[:, h * head:(h + 1) * head] = dq_scr[h]


def flash_backward(reach, own, queries, out_grad, key_stack, value_stack, lse, delta,
                   *, heads, head, scale, interpret=False):
    rows, width = queries.shape
    blocks = key_stack.shape[0]
    kv_width = key_stack.shape[2]
    groups = width // (heads * head)
    kernel = functools.partial(_bwd_kernel, heads=heads, head=head, scale=scale)
    grid_spec = pltpu.PrefetchScalarGridSpec(
        num_scalar_prefetch=2,
        grid=(groups, blocks),
        in_specs=[
            pl.BlockSpec((rows, heads * head), lambda g, b, r, o: (0, g)),
            pl.BlockSpec((rows, heads * head), lambda g, b, r, o: (0, g)),
            pl.BlockSpec((1, rows, head), lambda g, b, r, o: (b, 0, g)),
            pl.BlockSpec((1, rows, head), lambda g, b, r, o: (b, 0, g)),
            pl.BlockSpec((heads, rows, 1), lambda g, b, r, o: (g, 0, 0)),
            pl.BlockSpec((heads, rows, 1), lambda g, b, r, o: (g, 0, 0)),
        ],
        out_specs=[
            pl.BlockSpec((rows, heads * head), lambda g, b, r, o: (0, g)),
            pl.BlockSpec((1, rows, head), lambda g, b, r, o: (b, 0, g)),
            pl.BlockSpec((1, rows, head), lambda g, b, r, o: (b, 0, g)),
        ],
        scratch_shapes=[pltpu.VMEM((heads, rows, head), jnp.float32)],
    )
    return pl.pallas_call(
        kernel,
        grid_spec=grid_spec,
        out_shape=[
            jax.ShapeDtypeStruct((rows, width), jnp.float32),
            jax.ShapeDtypeStruct((blocks, rows, kv_width), jnp.float32),
            jax.ShapeDtypeStruct((blocks, rows, kv_width), jnp.float32),
        ],
        compiler_params=pltpu.CompilerParams(dimension_semantics=("arbitrary", "arbitrary")),
        interpret=interpret,
    )(reach, own, queries, out_grad, key_stack, value_stack, lse, delta)


def body(query_input, key_input, value_input, out_grad, query_bias, key_bias, value_bias, parents):
    tree_count, row_count, query_width = query_input.shape
    key_width = key_input.shape[2]
    score_scale = HEAD ** (-0.5)
    group_size = Q_HEADS // KV_HEADS
    devices = lax.axis_size("ctx")
    device_index = lax.axis_index("ctx")
    raw_pair = jnp.stack([key_input, value_input], axis=2)
    gathered = lax.all_gather(raw_pair, "ctx", axis=1, tiled=True)
    ancestors = jax.vmap(ancestry)(parents)
    block_depth = jnp.sum(ancestors, axis=2) - 1.0
    offsets = jnp.arange(row_count, dtype=jnp.float32)
    all_places = block_depth[:, :, None] * row_count + offsets[None, None, :]
    own_places = lax.dynamic_index_in_dim(all_places, device_index, 1, keepdims=False)
    own_reach = lax.dynamic_index_in_dim(ancestors, device_index, 1, keepdims=False)
    queries = rotate(
        (query_input.astype(jnp.float32) + query_bias).reshape(
            tree_count, row_count, Q_HEADS, HEAD
        ),
        own_places,
        1.0,
    ).astype(jnp.bfloat16)
    tree_length = row_count * devices
    flat_places = all_places.reshape(tree_count, tree_length)
    key_piece = rotate(
        (gathered[:, :, 0].astype(jnp.float32) + key_bias).reshape(
            tree_count, tree_length, KV_HEADS, HEAD
        ),
        flat_places,
        1.0,
    ).astype(jnp.bfloat16)
    value_piece = (
        (gathered[:, :, 1].astype(jnp.float32) + value_bias)
        .astype(jnp.bfloat16)
        .reshape(tree_count, tree_length, KV_HEADS, HEAD)
    )
    reach_flags = (own_reach[0] > 0.5).astype(jnp.int32)
    own_block = jnp.reshape(device_index, (1,)).astype(jnp.int32)
    flat_queries = queries.reshape(row_count, query_width)
    flat_grads = out_grad.reshape(row_count, query_width)
    key_stack = key_piece.reshape(devices, row_count, key_width)
    value_stack = value_piece.reshape(devices, row_count, key_width)
    out_rows, log_total = flash_forward(
        reach_flags, own_block, flat_queries, key_stack, value_stack,
        heads=group_size, head=HEAD, scale=score_scale,
    )
    row_delta = jnp.sum(
        (flat_grads.astype(jnp.float32) * out_rows.astype(jnp.float32)).reshape(
            row_count, Q_HEADS, HEAD
        ),
        axis=-1,
    )
    row_delta = jnp.transpose(row_delta, (1, 0))[:, :, None]
    query_sum, key_parts, value_parts = flash_backward(
        reach_flags, own_block, flat_queries, flat_grads, key_stack, value_stack,
        log_total, row_delta, heads=group_size, head=HEAD, scale=score_scale,
    )
    key_parts = rotate(
        key_parts.reshape(devices, row_count, KV_HEADS, HEAD), all_places[0], -1.0
    ).reshape(devices, row_count, key_width)
    key_total = jnp.sum(key_parts, axis=(0, 1))
    value_total = jnp.sum(value_parts, axis=(0, 1))
    stacked = jnp.stack([key_parts, value_parts], axis=2).astype(jnp.bfloat16)
    stacked = stacked.reshape(devices, tree_count, row_count, 2, key_width)
    own_grads = lax.psum_scatter(
        stacked.reshape(tree_count, devices * row_count, 2, key_width),
        "ctx", scatter_dimension=1, tiled=True,
    ).astype(jnp.float32)
    key_full = own_grads[:, :, 0]
    value_full = own_grads[:, :, 1]
    query_full = rotate(
        query_sum.reshape(tree_count, row_count, Q_HEADS, HEAD), own_places, -1.0
    ).reshape(tree_count, row_count, query_width)
    attended = out_rows.reshape(tree_count, row_count, query_width)
    query_total = jnp.sum(query_full, axis=(0, 1))
    query_total, key_total, value_total = lax.psum(
        (query_total, key_total, value_total), ("dp", "ctx")
    )
    return (attended, query_full, key_full, value_full, query_total, key_total, value_total)


def solution(mesh):
    placed = (
        P("dp", "ctx", None),
        P("dp", "ctx", None),
        P("dp", "ctx", None),
        P("dp", "ctx", None),
        P(),
        P(),
        P(),
        P("dp", None),
    )
    return jax.shard_map(
        body,
        mesh=mesh,
        in_specs=placed,
        out_specs=(
            P("dp", "ctx", None),
            P("dp", "ctx", None),
            P("dp", "ctx", None),
            P("dp", "ctx", None),
            P(),
            P(),
            P(),
        ),
        check_vma=False,
    )
```

```python
import functools
import math

import jax
import jax.numpy as jnp
from jax import lax
from jax.experimental import pallas as pl
from jax.experimental.pallas import tpu as pltpu
from jax.sharding import PartitionSpec as P

Q_HEADS = 64
KV_HEADS = 8
HEAD = 128


LOG_BASE = math.log(1000000.0)
NEG_LARGE = -1e30


def ancestry(parent_list):
    block_count = parent_list.shape[0]
    block_ids = jnp.arange(block_count, dtype=jnp.int32)
    step_matrix = ((parent_list[:, None] == block_ids[None, :]) & (block_ids[:, None] > 0)).astype(
        jnp.float32
    )
    reach = jnp.eye(block_count, dtype=jnp.float32) + step_matrix
    steps = 1
    while steps < block_count:
        reach = jnp.minimum(jnp.dot(reach, reach, precision=lax.Precision.HIGHEST), 1.0)
        steps *= 2
    return reach


def rotate(values, places, direction):
    half_width = values.shape[-1] // 2
    frequency = jnp.exp(
        jnp.arange(half_width, dtype=jnp.float32) * (-2.0 * LOG_BASE / values.shape[-1])
    )
    angles = places[..., None] * frequency
    cosine = jnp.cos(angles)[..., None, :]
    sine_part = direction * jnp.sin(angles)[..., None, :]
    first_half = values[..., :half_width]
    second = values[..., half_width:]
    return jnp.concatenate(
        [first_half * cosine - second * sine_part, second * cosine + first_half * sine_part],
        axis=-1,
    )


def allowed_tiles(reach_values, same_block, row_count):
    row_ids = jnp.arange(row_count, dtype=jnp.int32)
    causal = row_ids[None, :] <= row_ids[:, None]
    return (reach_values[:, None, None] > 0.5) & (jnp.logical_not(same_block) | causal)[None]


def _visible(block, own, rows):
    row_ids = lax.broadcasted_iota(jnp.int32, (rows, rows), 0)
    col_ids = lax.broadcasted_iota(jnp.int32, (rows, rows), 1)
    return jnp.logical_or(block != own, col_ids <= row_ids)


def _fwd_kernel(reach_ref, own_ref, q_ref, k_ref, v_ref, o_ref, lse_ref, m_scr, l_scr, acc_scr,
                *, heads, head, scale):
    block = pl.program_id(1)
    last = pl.num_programs(1) - 1
    rows = q_ref.shape[0]

    @pl.when(block == 0)
    def _():
        m_scr[...] = jnp.full(m_scr.shape, NEG_LARGE, jnp.float32)
        l_scr[...] = jnp.zeros(l_scr.shape, jnp.float32)
        acc_scr[...] = jnp.zeros(acc_scr.shape, jnp.float32)

    def step(masked):
        key_t = k_ref[0].T
        value = v_ref[0]
        mask = _visible(block, own_ref[0], rows) if masked else None
        for h in range(heads):
            query = q_ref[:, h * head:(h + 1) * head]
            scores = jnp.dot(query, key_t, preferred_element_type=jnp.float32) * scale
            if masked:
                scores = jnp.where(mask, scores, NEG_LARGE)
            m_prev = m_scr[h]
            m_new = jnp.maximum(m_prev, jnp.max(scores, axis=-1, keepdims=True))
            weights = jnp.exp(scores - m_new)
            if masked:
                weights = jnp.where(mask, weights, 0.0)
            factor = jnp.exp(m_prev - m_new)
            l_scr[h] = l_scr[h] * factor + jnp.sum(weights, axis=-1, keepdims=True)
            mixed = jnp.dot(weights.astype(jnp.bfloat16), value, preferred_element_type=jnp.float32)
            acc_scr[h] = acc_scr[h] * factor + mixed
            m_scr[h] = m_new

    @pl.when(jnp.logical_and(reach_ref[block] > 0, block == own_ref[0]))
    def _():
        step(True)

    @pl.when(jnp.logical_and(reach_ref[block] > 0, block != own_ref[0]))
    def _():
        step(False)

    @pl.when(block == last)
    def _():
        for h in range(heads):
            total = l_scr[h]
            o_ref[:, h * head:(h + 1) * head] = (acc_scr[h] / total).astype(o_ref.dtype)
            lse_ref[h] = m_scr[h] + jnp.log(total)


def flash_forward(reach, own, queries, key_stack, value_stack, *, heads, head, scale, interpret=False):
    rows, width = queries.shape
    blocks = key_stack.shape[0]
    groups = width // (heads * head)
    kernel = functools.partial(_fwd_kernel, heads=heads, head=head, scale=scale)
    grid_spec = pltpu.PrefetchScalarGridSpec(
        num_scalar_prefetch=2,
        grid=(groups, blocks),
        in_specs=[
            pl.BlockSpec((rows, heads * head), lambda g, b, r, o: (0, g)),
            pl.BlockSpec((1, rows, head), lambda g, b, r, o: (b, 0, g)),
            pl.BlockSpec((1, rows, head), lambda g, b, r, o: (b, 0, g)),
        ],
        out_specs=[
            pl.BlockSpec((rows, heads * head), lambda g, b, r, o: (0, g)),
            pl.BlockSpec((heads, rows, 1), lambda g, b, r, o: (g, 0, 0)),
        ],
        scratch_shapes=[
            pltpu.VMEM((heads, rows, 1), jnp.float32),
            pltpu.VMEM((heads, rows, 1), jnp.float32),
            pltpu.VMEM((heads, rows, head), jnp.float32),
        ],
    )
    return pl.pallas_call(
        kernel,
        grid_spec=grid_spec,
        out_shape=[
            jax.ShapeDtypeStruct((rows, width), jnp.bfloat16),
            jax.ShapeDtypeStruct((groups * heads, rows, 1), jnp.float32),
        ],
        compiler_params=pltpu.CompilerParams(dimension_semantics=("arbitrary", "arbitrary")),
        interpret=interpret,
    )(reach, own, queries, key_stack, value_stack)


def _bwd_kernel(reach_ref, own_ref, q_ref, do_ref, k_ref, v_ref, lse_ref, delta_ref,
                dq_ref, dk_ref, dv_ref, dq_scr, *, heads, head, scale):
    block = pl.program_id(1)
    last = pl.num_programs(1) - 1
    rows = q_ref.shape[0]

    @pl.when(block == 0)
    def _():
        dq_scr[...] = jnp.zeros(dq_scr.shape, jnp.float32)

    def step(masked):
        key = k_ref[0]
        key_t = key.T
        value_t = v_ref[0].T
        mask = _visible(block, own_ref[0], rows) if masked else None
        key_acc = jnp.zeros((rows, head), jnp.float32)
        value_acc = jnp.zeros((rows, head), jnp.float32)
        for h in range(heads):
            query = q_ref[:, h * head:(h + 1) * head]
            grad = do_ref[:, h * head:(h + 1) * head]
            scores = jnp.dot(query, key_t, preferred_element_type=jnp.float32) * scale
            if masked:
                scores = jnp.where(mask, scores, NEG_LARGE)
            probs = jnp.exp(scores - lse_ref[h])
            if masked:
                probs = jnp.where(mask, probs, 0.0)
            grad_probs = jnp.dot(grad, value_t, preferred_element_type=jnp.float32)
            grad_low = (probs * (grad_probs - delta_ref[h])).astype(jnp.bfloat16)
            dq_scr[h] = dq_scr[h] + jnp.dot(grad_low, key, preferred_element_type=jnp.float32) * scale
            key_acc = key_acc + lax.dot_general(grad_low, query, (((0,), (0,)), ((), ())),
                                                preferred_element_type=jnp.float32)
            value_acc = value_acc + lax.dot_general(probs.astype(jnp.bfloat16), grad,
                                                    (((0,), (0,)), ((), ())),
                                                    preferred_element_type=jnp.float32)
        dk_ref[0] = key_acc * scale
        dv_ref[0] = value_acc

    @pl.when(jnp.logical_and(reach_ref[block] > 0, block == own_ref[0]))
    def _():
        step(True)

    @pl.when(jnp.logical_and(reach_ref[block] > 0, block != own_ref[0]))
    def _():
        step(False)

    @pl.when(reach_ref[block] == 0)
    def _():
        dk_ref[...] = jnp.zeros(dk_ref.shape, jnp.float32)
        dv_ref[...] = jnp.zeros(dv_ref.shape, jnp.float32)

    @pl.when(block == last)
    def _():
        for h in range(heads):
            dq_ref[:, h * head:(h + 1) * head] = dq_scr[h]


def flash_backward(reach, own, queries, out_grad, key_stack, value_stack, lse, delta,
                   *, heads, head, scale, interpret=False):
    rows, width = queries.shape
    blocks = key_stack.shape[0]
    kv_width = key_stack.shape[2]
    groups = width // (heads * head)
    kernel = functools.partial(_bwd_kernel, heads=heads, head=head, scale=scale)
    grid_spec = pltpu.PrefetchScalarGridSpec(
        num_scalar_prefetch=2,
        grid=(groups, blocks),
        in_specs=[
            pl.BlockSpec((rows, heads * head), lambda g, b, r, o: (0, g)),
            pl.BlockSpec((rows, heads * head), lambda g, b, r, o: (0, g)),
            pl.BlockSpec((1, rows, head), lambda g, b, r, o: (b, 0, g)),
            pl.BlockSpec((1, rows, head), lambda g, b, r, o: (b, 0, g)),
            pl.BlockSpec((heads, rows, 1), lambda g, b, r, o: (g, 0, 0)),
            pl.BlockSpec((heads, rows, 1), lambda g, b, r, o: (g, 0, 0)),
        ],
        out_specs=[
            pl.BlockSpec((rows, heads * head), lambda g, b, r, o: (0, g)),
            pl.BlockSpec((1, rows, head), lambda g, b, r, o: (b, 0, g)),
            pl.BlockSpec((1, rows, head), lambda g, b, r, o: (b, 0, g)),
        ],
        scratch_shapes=[pltpu.VMEM((heads, rows, head), jnp.float32)],
    )
    return pl.pallas_call(
        kernel,
        grid_spec=grid_spec,
        out_shape=[
            jax.ShapeDtypeStruct((rows, width), jnp.float32),
            jax.ShapeDtypeStruct((blocks, rows, kv_width), jnp.float32),
            jax.ShapeDtypeStruct((blocks, rows, kv_width), jnp.float32),
        ],
        compiler_params=pltpu.CompilerParams(dimension_semantics=("arbitrary", "arbitrary")),
        interpret=interpret,
    )(reach, own, queries, out_grad, key_stack, value_stack, lse, delta)


def body(query_input, key_input, value_input, out_grad, query_bias, key_bias, value_bias, parents):
    tree_count, row_count, query_width = query_input.shape
    key_width = key_input.shape[2]
    score_scale = HEAD ** (-0.5)
    group_size = Q_HEADS // KV_HEADS
    devices = lax.axis_size("ctx")
    device_index = lax.axis_index("ctx")
    raw_pair = jnp.stack([key_input, value_input], axis=2)
    gathered = lax.all_gather(raw_pair, "ctx", axis=1, tiled=True)
    ancestors = jax.vmap(ancestry)(parents)
    block_depth = jnp.sum(ancestors, axis=2) - 1.0
    offsets = jnp.arange(row_count, dtype=jnp.float32)
    all_places = block_depth[:, :, None] * row_count + offsets[None, None, :]
    own_places = lax.dynamic_index_in_dim(all_places, device_index, 1, keepdims=False)
    own_reach = lax.dynamic_index_in_dim(ancestors, device_index, 1, keepdims=False)
    queries = rotate(
        (query_input.astype(jnp.float32) + query_bias).reshape(
            tree_count, row_count, Q_HEADS, HEAD
        ),
        own_places,
        1.0,
    ).astype(jnp.bfloat16)
    tree_length = row_count * devices
    flat_places = all_places.reshape(tree_count, tree_length)
    key_piece = rotate(
        (gathered[:, :, 0].astype(jnp.float32) + key_bias).reshape(
            tree_count, tree_length, KV_HEADS, HEAD
        ),
        flat_places,
        1.0,
    ).astype(jnp.bfloat16)
    value_piece = (
        (gathered[:, :, 1].astype(jnp.float32) + value_bias)
        .astype(jnp.bfloat16)
        .reshape(tree_count, tree_length, KV_HEADS, HEAD)
    )
    reach_flags = (own_reach[0] > 0.5).astype(jnp.int32)
    own_block = jnp.reshape(device_index, (1,)).astype(jnp.int32)
    flat_queries = queries.reshape(row_count, query_width)
    flat_grads = out_grad.reshape(row_count, query_width)
    key_stack = key_piece.reshape(devices, row_count, key_width)
    value_stack = value_piece.reshape(devices, row_count, key_width)
    out_rows, log_total = flash_forward(
        reach_flags, own_block, flat_queries, key_stack, value_stack,
        heads=group_size, head=HEAD, scale=score_scale,
    )
    row_delta = jnp.sum(
        (flat_grads.astype(jnp.float32) * out_rows.astype(jnp.float32)).reshape(
            row_count, Q_HEADS, HEAD
        ),
        axis=-1,
    )
    row_delta = jnp.transpose(row_delta, (1, 0))[:, :, None]
    query_sum, key_parts, value_parts = flash_backward(
        reach_flags, own_block, flat_queries, flat_grads, key_stack, value_stack,
        log_total, row_delta, heads=group_size, head=HEAD, scale=score_scale,
    )
    key_parts = rotate(
        key_parts.reshape(devices, row_count, KV_HEADS, HEAD), all_places[0], -1.0
    ).reshape(devices, row_count, key_width)
    key_total = jnp.sum(key_parts, axis=(0, 1))
    value_total = jnp.sum(value_parts, axis=(0, 1))
    stacked = jnp.stack([key_parts, value_parts], axis=2).astype(jnp.bfloat16)
    stacked = stacked.reshape(devices, tree_count, row_count, 2, key_width)
    own_grads = lax.psum_scatter(
        stacked.reshape(tree_count, devices * row_count, 2, key_width),
        "ctx", scatter_dimension=1, tiled=True,
    ).astype(jnp.float32)
    key_full = own_grads[:, :, 0]
    value_full = own_grads[:, :, 1]
    query_full = rotate(
        query_sum.reshape(tree_count, row_count, Q_HEADS, HEAD), own_places, -1.0
    ).reshape(tree_count, row_count, query_width)
    attended = out_rows.reshape(tree_count, row_count, query_width)
    query_total = jnp.sum(query_full, axis=(0, 1))
    query_total, key_total, value_total = lax.psum(
        (query_total, key_total, value_total), ("dp", "ctx")
    )
    return (attended, query_full, key_full, value_full, query_total, key_total, value_total)


def solution(mesh):
    placed = (
        P("dp", "ctx", None),
        P("dp", "ctx", None),
        P("dp", "ctx", None),
        P("dp", "ctx", None),
        P(),
        P(),
        P(),
        P("dp", None),
    )
    return jax.shard_map(
        body,
        mesh=mesh,
        in_specs=placed,
        out_specs=(
            P("dp", "ctx", None),
            P("dp", "ctx", None),
            P("dp", "ctx", None),
            P("dp", "ctx", None),
            P(),
            P(),
            P(),
        ),
        check_vma=False,
    )
```

```python
import functools
import math

import jax
import jax.numpy as jnp
from jax import lax
from jax.experimental import pallas as pl
from jax.experimental.pallas import tpu as pltpu
from jax.sharding import PartitionSpec as P

Q_HEADS = 64
KV_HEADS = 8
HEAD = 128


LOG_BASE = math.log(1000000.0)
NEG_LARGE = -1e30


def ancestry(parent_list):
    block_count = parent_list.shape[0]
    block_ids = jnp.arange(block_count, dtype=jnp.int32)
    step_matrix = ((parent_list[:, None] == block_ids[None, :]) & (block_ids[:, None] > 0)).astype(
        jnp.float32
    )
    reach = jnp.eye(block_count, dtype=jnp.float32) + step_matrix
    steps = 1
    while steps < block_count:
        reach = jnp.minimum(jnp.dot(reach, reach, precision=lax.Precision.HIGHEST), 1.0)
        steps *= 2
    return reach


def rotate(values, places, direction):
    half_width = values.shape[-1] // 2
    frequency = jnp.exp(
        jnp.arange(half_width, dtype=jnp.float32) * (-2.0 * LOG_BASE / values.shape[-1])
    )
    angles = places[..., None] * frequency
    cosine = jnp.cos(angles)[..., None, :]
    sine_part = direction * jnp.sin(angles)[..., None, :]
    first_half = values[..., :half_width]
    second = values[..., half_width:]
    return jnp.concatenate(
        [first_half * cosine - second * sine_part, second * cosine + first_half * sine_part],
        axis=-1,
    )


def allowed_tiles(reach_values, same_block, row_count):
    row_ids = jnp.arange(row_count, dtype=jnp.int32)
    causal = row_ids[None, :] <= row_ids[:, None]
    return (reach_values[:, None, None] > 0.5) & (jnp.logical_not(same_block) | causal)[None]


def _diagonal_mask(heads, rows):
    row_ids = lax.broadcasted_iota(jnp.int32, (heads, rows, rows), 1)
    col_ids = lax.broadcasted_iota(jnp.int32, (heads, rows, rows), 2)
    return (col_ids <= row_ids).reshape(heads * rows, rows)


def _fwd_kernel(reach_ref, own_ref, q_ref, k_ref, v_ref, o_ref, lse_ref, m_scr, l_scr, acc_scr,
                *, heads, scale):
    block = pl.program_id(1)
    last = pl.num_programs(1) - 1
    rows = k_ref.shape[1]

    @pl.when(block == 0)
    def _():
        m_scr[...] = jnp.full(m_scr.shape, NEG_LARGE, jnp.float32)
        l_scr[...] = jnp.zeros(l_scr.shape, jnp.float32)
        acc_scr[...] = jnp.zeros(acc_scr.shape, jnp.float32)

    def step(masked):
        scores = lax.dot_general(q_ref[...], k_ref[0], (((1,), (1,)), ((), ())),
                                 preferred_element_type=jnp.float32) * scale
        if masked:
            mask = _diagonal_mask(heads, rows)
            scores = jnp.where(mask, scores, NEG_LARGE)
        m_prev = m_scr[...]
        m_new = jnp.maximum(m_prev, jnp.max(scores, axis=-1, keepdims=True))
        weights = jnp.exp(scores - m_new)
        if masked:
            weights = jnp.where(mask, weights, 0.0)
        factor = jnp.exp(m_prev - m_new)
        l_scr[...] = l_scr[...] * factor + jnp.sum(weights, axis=-1, keepdims=True)
        mixed = jnp.dot(weights.astype(jnp.bfloat16), v_ref[0], preferred_element_type=jnp.float32)
        acc_scr[...] = acc_scr[...] * factor + mixed
        m_scr[...] = m_new

    @pl.when(jnp.logical_and(reach_ref[block] > 0, block == own_ref[0]))
    def _():
        step(True)

    @pl.when(jnp.logical_and(reach_ref[block] > 0, block != own_ref[0]))
    def _():
        step(False)

    @pl.when(block == last)
    def _():
        total = l_scr[...]
        o_ref[...] = (acc_scr[...] / total).astype(o_ref.dtype)
        lse_ref[...] = (m_scr[...] + jnp.log(total))[:, :1]


def flash_forward(reach, own, queries, key_stack, value_stack, *, heads, scale, interpret=False):
    blocks, rows, kv_width = key_stack.shape
    head = queries.shape[1]
    groups = kv_width // head
    tall = heads * rows
    kernel = functools.partial(_fwd_kernel, heads=heads, scale=scale)
    grid_spec = pltpu.PrefetchScalarGridSpec(
        num_scalar_prefetch=2,
        grid=(groups, blocks),
        in_specs=[
            pl.BlockSpec((tall, head), lambda g, b, r, o: (g, 0)),
            pl.BlockSpec((1, rows, head), lambda g, b, r, o: (b, 0, g)),
            pl.BlockSpec((1, rows, head), lambda g, b, r, o: (b, 0, g)),
        ],
        out_specs=[
            pl.BlockSpec((tall, head), lambda g, b, r, o: (g, 0)),
            pl.BlockSpec((tall, 1), lambda g, b, r, o: (g, 0)),
        ],
        scratch_shapes=[
            pltpu.VMEM((tall, head), jnp.float32),
            pltpu.VMEM((tall, head), jnp.float32),
            pltpu.VMEM((tall, head), jnp.float32),
        ],
    )
    return pl.pallas_call(
        kernel,
        grid_spec=grid_spec,
        out_shape=[
            jax.ShapeDtypeStruct(queries.shape, jnp.bfloat16),
            jax.ShapeDtypeStruct((queries.shape[0], 1), jnp.float32),
        ],
        compiler_params=pltpu.CompilerParams(dimension_semantics=("arbitrary", "arbitrary")),
        interpret=interpret,
    )(reach, own, queries, key_stack, value_stack)


def _bwd_kernel(reach_ref, own_ref, q_ref, do_ref, k_ref, v_ref, lse_ref, delta_ref,
                dq_ref, dk_ref, dv_ref, dq_scr, *, heads, scale):
    block = pl.program_id(1)
    last = pl.num_programs(1) - 1
    rows = k_ref.shape[1]

    @pl.when(block == 0)
    def _():
        dq_scr[...] = jnp.zeros(dq_scr.shape, jnp.float32)

    def step(masked):
        query = q_ref[...]
        grad = do_ref[...]
        key = k_ref[0]
        scores = lax.dot_general(query, key, (((1,), (1,)), ((), ())),
                                 preferred_element_type=jnp.float32) * scale
        if masked:
            mask = _diagonal_mask(heads, rows)
            scores = jnp.where(mask, scores, NEG_LARGE)
        probs = jnp.exp(scores - lse_ref[...])
        if masked:
            probs = jnp.where(mask, probs, 0.0)
        grad_probs = lax.dot_general(grad, v_ref[0], (((1,), (1,)), ((), ())),
                                     preferred_element_type=jnp.float32)
        grad_low = (probs * (grad_probs - delta_ref[...])).astype(jnp.bfloat16)
        dq_scr[...] = dq_scr[...] + jnp.dot(grad_low, key, preferred_element_type=jnp.float32) * scale
        dk_ref[0] = lax.dot_general(grad_low, query, (((0,), (0,)), ((), ())),
                                    preferred_element_type=jnp.float32) * scale
        dv_ref[0] = lax.dot_general(probs.astype(jnp.bfloat16), grad, (((0,), (0,)), ((), ())),
                                    preferred_element_type=jnp.float32)

    @pl.when(jnp.logical_and(reach_ref[block] > 0, block == own_ref[0]))
    def _():
        step(True)

    @pl.when(jnp.logical_and(reach_ref[block] > 0, block != own_ref[0]))
    def _():
        step(False)

    @pl.when(reach_ref[block] == 0)
    def _():
        dk_ref[...] = jnp.zeros(dk_ref.shape, jnp.float32)
        dv_ref[...] = jnp.zeros(dv_ref.shape, jnp.float32)

    @pl.when(block == last)
    def _():
        dq_ref[...] = dq_scr[...]


def flash_backward(reach, own, queries, out_grad, key_stack, value_stack, lse, delta,
                   *, heads, scale, interpret=False):
    blocks, rows, kv_width = key_stack.shape
    head = queries.shape[1]
    groups = kv_width // head
    tall = heads * rows
    kernel = functools.partial(_bwd_kernel, heads=heads, scale=scale)
    grid_spec = pltpu.PrefetchScalarGridSpec(
        num_scalar_prefetch=2,
        grid=(groups, blocks),
        in_specs=[
            pl.BlockSpec((tall, head), lambda g, b, r, o: (g, 0)),
            pl.BlockSpec((tall, head), lambda g, b, r, o: (g, 0)),
            pl.BlockSpec((1, rows, head), lambda g, b, r, o: (b, 0, g)),
            pl.BlockSpec((1, rows, head), lambda g, b, r, o: (b, 0, g)),
            pl.BlockSpec((tall, 1), lambda g, b, r, o: (g, 0)),
            pl.BlockSpec((tall, 1), lambda g, b, r, o: (g, 0)),
        ],
        out_specs=[
            pl.BlockSpec((tall, head), lambda g, b, r, o: (g, 0)),
            pl.BlockSpec((1, rows, head), lambda g, b, r, o: (b, 0, g)),
            pl.BlockSpec((1, rows, head), lambda g, b, r, o: (b, 0, g)),
        ],
        scratch_shapes=[pltpu.VMEM((tall, head), jnp.float32)],
    )
    return pl.pallas_call(
        kernel,
        grid_spec=grid_spec,
        out_shape=[
            jax.ShapeDtypeStruct(queries.shape, jnp.float32),
            jax.ShapeDtypeStruct(key_stack.shape, jnp.float32),
            jax.ShapeDtypeStruct(key_stack.shape, jnp.float32),
        ],
        compiler_params=pltpu.CompilerParams(dimension_semantics=("arbitrary", "arbitrary")),
        interpret=interpret,
    )(reach, own, queries, out_grad, key_stack, value_stack, lse, delta)


def body(query_input, key_input, value_input, out_grad, query_bias, key_bias, value_bias, parents):
    tree_count, row_count, query_width = query_input.shape
    key_width = key_input.shape[2]
    score_scale = HEAD ** (-0.5)
    group_size = Q_HEADS // KV_HEADS
    devices = lax.axis_size("ctx")
    device_index = lax.axis_index("ctx")
    raw_pair = jnp.stack([key_input, value_input], axis=2)
    gathered = lax.all_gather(raw_pair, "ctx", axis=1, tiled=True)
    ancestors = jax.vmap(ancestry)(parents)
    block_depth = jnp.sum(ancestors, axis=2) - 1.0
    offsets = jnp.arange(row_count, dtype=jnp.float32)
    all_places = block_depth[:, :, None] * row_count + offsets[None, None, :]
    own_places = lax.dynamic_index_in_dim(all_places, device_index, 1, keepdims=False)
    own_reach = lax.dynamic_index_in_dim(ancestors, device_index, 1, keepdims=False)
    queries = rotate(
        (query_input.astype(jnp.float32) + query_bias).reshape(
            tree_count, row_count, Q_HEADS, HEAD
        ),
        own_places,
        1.0,
    ).astype(jnp.bfloat16)
    tree_length = row_count * devices
    flat_places = all_places.reshape(tree_count, tree_length)
    key_piece = rotate(
        (gathered[:, :, 0].astype(jnp.float32) + key_bias).reshape(
            tree_count, tree_length, KV_HEADS, HEAD
        ),
        flat_places,
        1.0,
    ).astype(jnp.bfloat16)
    value_piece = (
        (gathered[:, :, 1].astype(jnp.float32) + value_bias)
        .astype(jnp.bfloat16)
        .reshape(tree_count, tree_length, KV_HEADS, HEAD)
    )
    reach_flags = (own_reach[0] > 0.5).astype(jnp.int32)
    own_block = jnp.reshape(device_index, (1,)).astype(jnp.int32)
    tall_queries = jnp.transpose(queries.reshape(row_count, Q_HEADS, HEAD), (1, 0, 2)).reshape(
        Q_HEADS * row_count, HEAD
    )
    tall_grads = jnp.transpose(out_grad.reshape(row_count, Q_HEADS, HEAD), (1, 0, 2)).reshape(
        Q_HEADS * row_count, HEAD
    )
    key_stack = key_piece.reshape(devices, row_count, key_width)
    value_stack = value_piece.reshape(devices, row_count, key_width)
    tall_out, log_total = flash_forward(
        reach_flags, own_block, tall_queries, key_stack, value_stack,
        heads=group_size, scale=score_scale,
    )
    row_delta = jnp.sum(
        tall_grads.astype(jnp.float32) * tall_out.astype(jnp.float32), axis=-1, keepdims=True
    )
    tall_dq, key_parts, value_parts = flash_backward(
        reach_flags, own_block, tall_queries, tall_grads, key_stack, value_stack,
        log_total, row_delta, heads=group_size, scale=score_scale,
    )
    out_rows = jnp.transpose(tall_out.reshape(Q_HEADS, row_count, HEAD), (1, 0, 2))
    query_sum = jnp.transpose(tall_dq.reshape(Q_HEADS, row_count, HEAD), (1, 0, 2))
    key_parts = rotate(
        key_parts.reshape(devices, row_count, KV_HEADS, HEAD), all_places[0], -1.0
    ).reshape(devices, row_count, key_width)
    key_total = jnp.sum(key_parts, axis=(0, 1))
    value_total = jnp.sum(value_parts, axis=(0, 1))
    stacked = jnp.stack([key_parts, value_parts], axis=2).astype(jnp.bfloat16)
    stacked = stacked.reshape(devices, tree_count, row_count, 2, key_width)
    own_grads = lax.psum_scatter(
        stacked.reshape(tree_count, devices * row_count, 2, key_width),
        "ctx", scatter_dimension=1, tiled=True,
    ).astype(jnp.float32)
    key_full = own_grads[:, :, 0]
    value_full = own_grads[:, :, 1]
    query_full = rotate(
        query_sum.reshape(tree_count, row_count, Q_HEADS, HEAD), own_places, -1.0
    ).reshape(tree_count, row_count, query_width)
    attended = out_rows.reshape(tree_count, row_count, query_width)
    query_total = jnp.sum(query_full, axis=(0, 1))
    query_total, key_total, value_total = lax.psum(
        (query_total, key_total, value_total), ("dp", "ctx")
    )
    return (attended, query_full, key_full, value_full, query_total, key_total, value_total)


def solution(mesh):
    placed = (
        P("dp", "ctx", None),
        P("dp", "ctx", None),
        P("dp", "ctx", None),
        P("dp", "ctx", None),
        P(),
        P(),
        P(),
        P("dp", None),
    )
    return jax.shard_map(
        body,
        mesh=mesh,
        in_specs=placed,
        out_specs=(
            P("dp", "ctx", None),
            P("dp", "ctx", None),
            P("dp", "ctx", None),
            P("dp", "ctx", None),
            P(),
            P(),
            P(),
        ),
        check_vma=False,
    )
```

```python
import functools
import math

import jax
import jax.numpy as jnp
from jax import lax
from jax.experimental import pallas as pl
from jax.experimental.pallas import tpu as pltpu
from jax.sharding import PartitionSpec as P

Q_HEADS = 64
KV_HEADS = 8
HEAD = 128


LOG_BASE = math.log(1000000.0)
NEG_LARGE = -1e30


def ancestry(parent_list):
    block_count = parent_list.shape[0]
    block_ids = jnp.arange(block_count, dtype=jnp.int32)
    step_matrix = ((parent_list[:, None] == block_ids[None, :]) & (block_ids[:, None] > 0)).astype(
        jnp.float32
    )
    reach = jnp.eye(block_count, dtype=jnp.float32) + step_matrix
    steps = 1
    while steps < block_count:
        reach = jnp.minimum(jnp.dot(reach, reach, precision=lax.Precision.HIGHEST), 1.0)
        steps *= 2
    return reach


def rotate(values, places, direction):
    half_width = values.shape[-1] // 2
    frequency = jnp.exp(
        jnp.arange(half_width, dtype=jnp.float32) * (-2.0 * LOG_BASE / values.shape[-1])
    )
    angles = places[..., None] * frequency
    cosine = jnp.cos(angles)[..., None, :]
    sine_part = direction * jnp.sin(angles)[..., None, :]
    first_half = values[..., :half_width]
    second = values[..., half_width:]
    return jnp.concatenate(
        [first_half * cosine - second * sine_part, second * cosine + first_half * sine_part],
        axis=-1,
    )


def allowed_tiles(reach_values, same_block, row_count):
    row_ids = jnp.arange(row_count, dtype=jnp.int32)
    causal = row_ids[None, :] <= row_ids[:, None]
    return (reach_values[:, None, None] > 0.5) & (jnp.logical_not(same_block) | causal)[None]


def _diagonal_mask(heads, rows):
    row_ids = lax.broadcasted_iota(jnp.int32, (heads, rows, rows), 1)
    col_ids = lax.broadcasted_iota(jnp.int32, (heads, rows, rows), 2)
    return (col_ids <= row_ids).reshape(heads * rows, rows)


def _fwd_kernel(reach_ref, own_ref, q_ref, k_ref, v_ref, o_ref, lse_ref, m_scr, l_scr, acc_scr,
                *, heads, scale):
    block = pl.program_id(1)
    last = pl.num_programs(1) - 1
    rows = k_ref.shape[1]

    @pl.when(block == 0)
    def _():
        m_scr[...] = jnp.full(m_scr.shape, NEG_LARGE, jnp.float32)
        l_scr[...] = jnp.zeros(l_scr.shape, jnp.float32)
        acc_scr[...] = jnp.zeros(acc_scr.shape, jnp.float32)

    def step(masked):
        scores = lax.dot_general(q_ref[...], k_ref[0], (((1,), (1,)), ((), ())),
                                 preferred_element_type=jnp.float32) * scale
        if masked:
            mask = _diagonal_mask(heads, rows)
            scores = jnp.where(mask, scores, NEG_LARGE)
        m_prev = m_scr[...]
        m_new = jnp.maximum(m_prev, jnp.max(scores, axis=-1, keepdims=True))
        weights = jnp.exp(scores - m_new)
        if masked:
            weights = jnp.where(mask, weights, 0.0)
        factor = jnp.exp(m_prev - m_new)
        l_scr[...] = l_scr[...] * factor + jnp.sum(weights, axis=-1, keepdims=True)
        mixed = jnp.dot(weights.astype(jnp.bfloat16), v_ref[0], preferred_element_type=jnp.float32)
        acc_scr[...] = acc_scr[...] * factor + mixed
        m_scr[...] = m_new

    @pl.when(jnp.logical_and(reach_ref[block] > 0, block == own_ref[0]))
    def _():
        step(True)

    @pl.when(jnp.logical_and(reach_ref[block] > 0, block != own_ref[0]))
    def _():
        step(False)

    @pl.when(block == last)
    def _():
        total = l_scr[...]
        o_ref[...] = (acc_scr[...] / total).astype(o_ref.dtype)
        lse_ref[...] = (m_scr[...] + jnp.log(total))[:, :1]


def flash_forward(reach, own, queries, key_stack, value_stack, *, heads, scale, interpret=False):
    blocks, rows, kv_width = key_stack.shape
    head = queries.shape[1]
    groups = kv_width // head
    tall = heads * rows
    kernel = functools.partial(_fwd_kernel, heads=heads, scale=scale)
    grid_spec = pltpu.PrefetchScalarGridSpec(
        num_scalar_prefetch=2,
        grid=(groups, blocks),
        in_specs=[
            pl.BlockSpec((tall, head), lambda g, b, r, o: (g, 0)),
            pl.BlockSpec((1, rows, head), lambda g, b, r, o: (b, 0, g)),
            pl.BlockSpec((1, rows, head), lambda g, b, r, o: (b, 0, g)),
        ],
        out_specs=[
            pl.BlockSpec((tall, head), lambda g, b, r, o: (g, 0)),
            pl.BlockSpec((tall, 1), lambda g, b, r, o: (g, 0)),
        ],
        scratch_shapes=[
            pltpu.VMEM((tall, head), jnp.float32),
            pltpu.VMEM((tall, head), jnp.float32),
            pltpu.VMEM((tall, head), jnp.float32),
        ],
    )
    return pl.pallas_call(
        kernel,
        grid_spec=grid_spec,
        out_shape=[
            jax.ShapeDtypeStruct(queries.shape, jnp.bfloat16),
            jax.ShapeDtypeStruct((queries.shape[0], 1), jnp.float32),
        ],
        compiler_params=pltpu.CompilerParams(dimension_semantics=("arbitrary", "arbitrary")),
        interpret=interpret,
    )(reach, own, queries, key_stack, value_stack)


def _bwd_kernel(reach_ref, own_ref, q_ref, do_ref, k_ref, v_ref, lse_ref, delta_ref,
                dq_ref, dkv_ref, dq_scr, *, heads, scale):
    block = pl.program_id(1)
    last = pl.num_programs(1) - 1
    rows = k_ref.shape[1]

    @pl.when(block == 0)
    def _():
        dq_scr[...] = jnp.zeros(dq_scr.shape, jnp.float32)

    def step(masked):
        query = q_ref[...]
        grad = do_ref[...]
        key = k_ref[0]
        scores = lax.dot_general(query, key, (((1,), (1,)), ((), ())),
                                 preferred_element_type=jnp.float32) * scale
        if masked:
            mask = _diagonal_mask(heads, rows)
            scores = jnp.where(mask, scores, NEG_LARGE)
        probs = jnp.exp(scores - lse_ref[...])
        if masked:
            probs = jnp.where(mask, probs, 0.0)
        grad_probs = lax.dot_general(grad, v_ref[0], (((1,), (1,)), ((), ())),
                                     preferred_element_type=jnp.float32)
        grad_low = (probs * (grad_probs - delta_ref[...])).astype(jnp.bfloat16)
        dq_scr[...] = dq_scr[...] + jnp.dot(grad_low, key, preferred_element_type=jnp.float32) * scale
        key_grad = lax.dot_general(grad_low, query, (((0,), (0,)), ((), ())),
                                   preferred_element_type=jnp.float32) * scale
        value_grad = lax.dot_general(probs.astype(jnp.bfloat16), grad, (((0,), (0,)), ((), ())),
                                     preferred_element_type=jnp.float32)
        dkv_ref[0, 0] = key_grad.astype(dkv_ref.dtype)
        dkv_ref[0, 1] = value_grad.astype(dkv_ref.dtype)

    @pl.when(jnp.logical_and(reach_ref[block] > 0, block == own_ref[0]))
    def _():
        step(True)

    @pl.when(jnp.logical_and(reach_ref[block] > 0, block != own_ref[0]))
    def _():
        step(False)

    @pl.when(reach_ref[block] == 0)
    def _():
        dkv_ref[...] = jnp.zeros(dkv_ref.shape, dkv_ref.dtype)

    @pl.when(block == last)
    def _():
        dq_ref[...] = dq_scr[...]


def flash_backward(reach, own, queries, out_grad, key_stack, value_stack, lse, delta,
                   *, heads, scale, interpret=False):
    blocks, rows, kv_width = key_stack.shape
    head = queries.shape[1]
    groups = kv_width // head
    tall = heads * rows
    kernel = functools.partial(_bwd_kernel, heads=heads, scale=scale)
    grid_spec = pltpu.PrefetchScalarGridSpec(
        num_scalar_prefetch=2,
        grid=(groups, blocks),
        in_specs=[
            pl.BlockSpec((tall, head), lambda g, b, r, o: (g, 0)),
            pl.BlockSpec((tall, head), lambda g, b, r, o: (g, 0)),
            pl.BlockSpec((1, rows, head), lambda g, b, r, o: (b, 0, g)),
            pl.BlockSpec((1, rows, head), lambda g, b, r, o: (b, 0, g)),
            pl.BlockSpec((tall, 1), lambda g, b, r, o: (g, 0)),
            pl.BlockSpec((tall, 1), lambda g, b, r, o: (g, 0)),
        ],
        out_specs=[
            pl.BlockSpec((tall, head), lambda g, b, r, o: (g, 0)),
            pl.BlockSpec((1, 2, rows, head), lambda g, b, r, o: (b, 0, 0, g)),
        ],
        scratch_shapes=[pltpu.VMEM((tall, head), jnp.float32)],
    )
    return pl.pallas_call(
        kernel,
        grid_spec=grid_spec,
        out_shape=[
            jax.ShapeDtypeStruct(queries.shape, jnp.float32),
            jax.ShapeDtypeStruct((blocks, 2, rows, kv_width), jnp.bfloat16),
        ],
        compiler_params=pltpu.CompilerParams(dimension_semantics=("arbitrary", "arbitrary")),
        interpret=interpret,
    )(reach, own, queries, out_grad, key_stack, value_stack, lse, delta)


def body(query_input, key_input, value_input, out_grad, query_bias, key_bias, value_bias, parents):
    tree_count, row_count, query_width = query_input.shape
    key_width = key_input.shape[2]
    score_scale = HEAD ** (-0.5)
    group_size = Q_HEADS // KV_HEADS
    devices = lax.axis_size("ctx")
    device_index = lax.axis_index("ctx")
    raw_pair = jnp.stack([key_input, value_input], axis=2)
    gathered = lax.all_gather(raw_pair, "ctx", axis=1, tiled=True)
    ancestors = jax.vmap(ancestry)(parents)
    block_depth = jnp.sum(ancestors, axis=2) - 1.0
    offsets = jnp.arange(row_count, dtype=jnp.float32)
    all_places = block_depth[:, :, None] * row_count + offsets[None, None, :]
    own_places = lax.dynamic_index_in_dim(all_places, device_index, 1, keepdims=False)
    own_reach = lax.dynamic_index_in_dim(ancestors, device_index, 1, keepdims=False)
    queries = rotate(
        (query_input.astype(jnp.float32) + query_bias).reshape(
            tree_count, row_count, Q_HEADS, HEAD
        ),
        own_places,
        1.0,
    ).astype(jnp.bfloat16)
    tree_length = row_count * devices
    flat_places = all_places.reshape(tree_count, tree_length)
    key_piece = rotate(
        (gathered[:, :, 0].astype(jnp.float32) + key_bias).reshape(
            tree_count, tree_length, KV_HEADS, HEAD
        ),
        flat_places,
        1.0,
    ).astype(jnp.bfloat16)
    value_piece = (
        (gathered[:, :, 1].astype(jnp.float32) + value_bias)
        .astype(jnp.bfloat16)
        .reshape(tree_count, tree_length, KV_HEADS, HEAD)
    )
    reach_flags = (own_reach[0] > 0.5).astype(jnp.int32)
    own_block = jnp.reshape(device_index, (1,)).astype(jnp.int32)
    tall_queries = jnp.transpose(queries.reshape(row_count, Q_HEADS, HEAD), (1, 0, 2)).reshape(
        Q_HEADS * row_count, HEAD
    )
    tall_grads = jnp.transpose(out_grad.reshape(row_count, Q_HEADS, HEAD), (1, 0, 2)).reshape(
        Q_HEADS * row_count, HEAD
    )
    key_stack = key_piece.reshape(devices, row_count, key_width)
    value_stack = value_piece.reshape(devices, row_count, key_width)
    tall_out, log_total = flash_forward(
        reach_flags, own_block, tall_queries, key_stack, value_stack,
        heads=group_size, scale=score_scale,
    )
    row_delta = jnp.sum(
        tall_grads.astype(jnp.float32) * tall_out.astype(jnp.float32), axis=-1, keepdims=True
    )
    tall_dq, grad_pairs = flash_backward(
        reach_flags, own_block, tall_queries, tall_grads, key_stack, value_stack,
        log_total, row_delta, heads=group_size, scale=score_scale,
    )
    out_rows = jnp.transpose(tall_out.reshape(Q_HEADS, row_count, HEAD), (1, 0, 2))
    query_sum = jnp.transpose(tall_dq.reshape(Q_HEADS, row_count, HEAD), (1, 0, 2))
    own_pair = lax.psum_scatter(
        grad_pairs.reshape(tree_count, devices * 2 * row_count, key_width),
        "ctx", scatter_dimension=1, tiled=True,
    ).reshape(tree_count, 2, row_count, key_width).astype(jnp.float32)
    key_full = rotate(
        own_pair[:, 0].reshape(tree_count, row_count, KV_HEADS, HEAD), own_places, -1.0
    ).reshape(tree_count, row_count, key_width)
    value_full = own_pair[:, 1]
    key_total = jnp.sum(key_full, axis=(0, 1))
    value_total = jnp.sum(value_full, axis=(0, 1))
    query_full = rotate(
        query_sum.reshape(tree_count, row_count, Q_HEADS, HEAD), own_places, -1.0
    ).reshape(tree_count, row_count, query_width)
    attended = out_rows.reshape(tree_count, row_count, query_width)
    query_total = jnp.sum(query_full, axis=(0, 1))
    query_total, key_total, value_total = lax.psum(
        (query_total, key_total, value_total), ("dp", "ctx")
    )
    return (attended, query_full, key_full, value_full, query_total, key_total, value_total)


def solution(mesh):
    placed = (
        P("dp", "ctx", None),
        P("dp", "ctx", None),
        P("dp", "ctx", None),
        P("dp", "ctx", None),
        P(),
        P(),
        P(),
        P("dp", None),
    )
    return jax.shard_map(
        body,
        mesh=mesh,
        in_specs=placed,
        out_specs=(
            P("dp", "ctx", None),
            P("dp", "ctx", None),
            P("dp", "ctx", None),
            P("dp", "ctx", None),
            P(),
            P(),
            P(),
        ),
        check_vma=False,
    )
```

```python
import functools
import math

import jax
import jax.numpy as jnp
from jax import lax
from jax.experimental import pallas as pl
from jax.experimental.pallas import tpu as pltpu
from jax.sharding import PartitionSpec as P

Q_HEADS = 64
KV_HEADS = 8
HEAD = 128


LOG_BASE = math.log(1000000.0)
NEG_LARGE = -1e30


def ancestry(parent_list):
    block_count = parent_list.shape[0]
    block_ids = jnp.arange(block_count, dtype=jnp.int32)
    step_matrix = ((parent_list[:, None] == block_ids[None, :]) & (block_ids[:, None] > 0)).astype(
        jnp.float32
    )
    reach = jnp.eye(block_count, dtype=jnp.float32) + step_matrix
    steps = 1
    while steps < block_count:
        reach = jnp.minimum(jnp.dot(reach, reach, precision=lax.Precision.HIGHEST), 1.0)
        steps *= 2
    return reach


def rotate(values, places, direction):
    half_width = values.shape[-1] // 2
    frequency = jnp.exp(
        jnp.arange(half_width, dtype=jnp.float32) * (-2.0 * LOG_BASE / values.shape[-1])
    )
    angles = places[..., None] * frequency
    cosine = jnp.cos(angles)[..., None, :]
    sine_part = direction * jnp.sin(angles)[..., None, :]
    first_half = values[..., :half_width]
    second = values[..., half_width:]
    return jnp.concatenate(
        [first_half * cosine - second * sine_part, second * cosine + first_half * sine_part],
        axis=-1,
    )


def allowed_tiles(reach_values, same_block, row_count):
    row_ids = jnp.arange(row_count, dtype=jnp.int32)
    causal = row_ids[None, :] <= row_ids[:, None]
    return (reach_values[:, None, None] > 0.5) & (jnp.logical_not(same_block) | causal)[None]


def _diagonal_mask(heads, rows):
    row_ids = lax.broadcasted_iota(jnp.int32, (heads, rows, rows), 1)
    col_ids = lax.broadcasted_iota(jnp.int32, (heads, rows, rows), 2)
    return (col_ids <= row_ids).reshape(heads * rows, rows)


def _fwd_kernel(reach_ref, own_ref, q_ref, k_ref, v_ref, o_ref, lse_ref, m_scr, l_scr, acc_scr,
                *, heads, scale):
    block = pl.program_id(1)
    last = pl.num_programs(1) - 1
    rows = k_ref.shape[1]

    @pl.when(block == 0)
    def _():
        m_scr[...] = jnp.full(m_scr.shape, NEG_LARGE, jnp.float32)
        l_scr[...] = jnp.zeros(l_scr.shape, jnp.float32)
        acc_scr[...] = jnp.zeros(acc_scr.shape, jnp.float32)

    def step(masked):
        scores = lax.dot_general(q_ref[...], k_ref[0], (((1,), (1,)), ((), ())),
                                 preferred_element_type=jnp.float32) * scale
        if masked:
            mask = _diagonal_mask(heads, rows)
            scores = jnp.where(mask, scores, NEG_LARGE)
        m_prev = m_scr[...]
        m_new = jnp.maximum(m_prev, jnp.max(scores, axis=-1, keepdims=True))
        weights = jnp.exp(scores - m_new)
        if masked:
            weights = jnp.where(mask, weights, 0.0)
        factor = jnp.exp(m_prev - m_new)
        l_scr[...] = l_scr[...] * factor + jnp.sum(weights, axis=-1, keepdims=True)
        mixed = jnp.dot(weights.astype(jnp.bfloat16), v_ref[0], preferred_element_type=jnp.float32)
        acc_scr[...] = acc_scr[...] * factor + mixed
        m_scr[...] = m_new

    @pl.when(jnp.logical_and(reach_ref[block] > 0, block == own_ref[0]))
    def _():
        step(True)

    @pl.when(jnp.logical_and(reach_ref[block] > 0, block != own_ref[0]))
    def _():
        step(False)

    @pl.when(block == last)
    def _():
        total = l_scr[...]
        o_ref[...] = (acc_scr[...] / total).astype(o_ref.dtype)
        lse_ref[...] = (m_scr[...] + jnp.log(total))[:, :1]


def flash_forward(reach, own, queries, key_stack, value_stack, *, heads, scale, interpret=False):
    blocks, rows, kv_width = key_stack.shape
    head = queries.shape[1]
    groups = kv_width // head
    tall = heads * rows
    kernel = functools.partial(_fwd_kernel, heads=heads, scale=scale)
    grid_spec = pltpu.PrefetchScalarGridSpec(
        num_scalar_prefetch=2,
        grid=(groups, blocks),
        in_specs=[
            pl.BlockSpec((tall, head), lambda g, b, r, o: (g, 0)),
            pl.BlockSpec((1, rows, head), lambda g, b, r, o: (b, 0, g)),
            pl.BlockSpec((1, rows, head), lambda g, b, r, o: (b, 0, g)),
        ],
        out_specs=[
            pl.BlockSpec((tall, head), lambda g, b, r, o: (g, 0)),
            pl.BlockSpec((tall, 1), lambda g, b, r, o: (g, 0)),
        ],
        scratch_shapes=[
            pltpu.VMEM((tall, head), jnp.float32),
            pltpu.VMEM((tall, head), jnp.float32),
            pltpu.VMEM((tall, head), jnp.float32),
        ],
    )
    return pl.pallas_call(
        kernel,
        grid_spec=grid_spec,
        out_shape=[
            jax.ShapeDtypeStruct(queries.shape, jnp.bfloat16),
            jax.ShapeDtypeStruct((queries.shape[0], 1), jnp.float32),
        ],
        compiler_params=pltpu.CompilerParams(dimension_semantics=("arbitrary", "arbitrary")),
        interpret=interpret,
    )(reach, own, queries, key_stack, value_stack)


def _bwd_kernel(reach_ref, own_ref, q_ref, do_ref, k_ref, v_ref, lse_ref, delta_ref,
                dq_ref, dkv_ref, dq_scr, *, heads, scale):
    block = pl.program_id(1)
    last = pl.num_programs(1) - 1
    rows = k_ref.shape[1]

    @pl.when(block == 0)
    def _():
        dq_scr[...] = jnp.zeros(dq_scr.shape, jnp.float32)

    def step(masked):
        query = q_ref[...]
        grad = do_ref[...]
        key = k_ref[0]
        scores = lax.dot_general(query, key, (((1,), (1,)), ((), ())),
                                 preferred_element_type=jnp.float32) * scale
        if masked:
            mask = _diagonal_mask(heads, rows)
            scores = jnp.where(mask, scores, NEG_LARGE)
        probs = jnp.exp(scores - lse_ref[...])
        if masked:
            probs = jnp.where(mask, probs, 0.0)
        grad_probs = lax.dot_general(grad, v_ref[0], (((1,), (1,)), ((), ())),
                                     preferred_element_type=jnp.float32)
        grad_low = (probs * (grad_probs - delta_ref[...])).astype(jnp.bfloat16)
        dq_scr[...] = dq_scr[...] + jnp.dot(grad_low, key, preferred_element_type=jnp.float32) * scale
        key_grad = lax.dot_general(grad_low, query, (((0,), (0,)), ((), ())),
                                   preferred_element_type=jnp.float32) * scale
        value_grad = lax.dot_general(probs.astype(jnp.bfloat16), grad, (((0,), (0,)), ((), ())),
                                     preferred_element_type=jnp.float32)
        dkv_ref[0, 0] = key_grad.astype(dkv_ref.dtype)
        dkv_ref[0, 1] = value_grad.astype(dkv_ref.dtype)

    @pl.when(jnp.logical_and(reach_ref[block] > 0, block == own_ref[0]))
    def _():
        step(True)

    @pl.when(jnp.logical_and(reach_ref[block] > 0, block != own_ref[0]))
    def _():
        step(False)

    @pl.when(reach_ref[block] == 0)
    def _():
        dkv_ref[...] = jnp.zeros(dkv_ref.shape, dkv_ref.dtype)

    @pl.when(block == last)
    def _():
        dq_ref[...] = dq_scr[...]


def flash_backward(reach, own, queries, out_grad, key_stack, value_stack, lse, delta,
                   *, heads, scale, interpret=False):
    blocks, rows, kv_width = key_stack.shape
    head = queries.shape[1]
    groups = kv_width // head
    tall = heads * rows
    kernel = functools.partial(_bwd_kernel, heads=heads, scale=scale)
    grid_spec = pltpu.PrefetchScalarGridSpec(
        num_scalar_prefetch=2,
        grid=(groups, blocks),
        in_specs=[
            pl.BlockSpec((tall, head), lambda g, b, r, o: (g, 0)),
            pl.BlockSpec((tall, head), lambda g, b, r, o: (g, 0)),
            pl.BlockSpec((1, rows, head), lambda g, b, r, o: (b, 0, g)),
            pl.BlockSpec((1, rows, head), lambda g, b, r, o: (b, 0, g)),
            pl.BlockSpec((tall, 1), lambda g, b, r, o: (g, 0)),
            pl.BlockSpec((tall, 1), lambda g, b, r, o: (g, 0)),
        ],
        out_specs=[
            pl.BlockSpec((tall, head), lambda g, b, r, o: (g, 0)),
            pl.BlockSpec((1, 2, rows, head), lambda g, b, r, o: (b, 0, 0, g)),
        ],
        scratch_shapes=[pltpu.VMEM((tall, head), jnp.float32)],
    )
    return pl.pallas_call(
        kernel,
        grid_spec=grid_spec,
        out_shape=[
            jax.ShapeDtypeStruct(queries.shape, jnp.float32),
            jax.ShapeDtypeStruct((blocks, 2, rows, kv_width), jnp.bfloat16),
        ],
        compiler_params=pltpu.CompilerParams(dimension_semantics=("arbitrary", "arbitrary")),
        interpret=interpret,
    )(reach, own, queries, out_grad, key_stack, value_stack, lse, delta)


def body(query_input, key_input, value_input, out_grad, query_bias, key_bias, value_bias, parents):
    tree_count, row_count, query_width = query_input.shape
    key_width = key_input.shape[2]
    score_scale = HEAD ** (-0.5)
    group_size = Q_HEADS // KV_HEADS
    devices = lax.axis_size("ctx")
    device_index = lax.axis_index("ctx")
    raw_pair = jnp.stack([key_input, value_input], axis=2)
    gathered = lax.all_gather(raw_pair, "ctx", axis=1, tiled=True)
    ancestors = jax.vmap(ancestry)(parents)
    block_depth = jnp.sum(ancestors, axis=2) - 1.0
    offsets = jnp.arange(row_count, dtype=jnp.float32)
    all_places = block_depth[:, :, None] * row_count + offsets[None, None, :]
    own_places = lax.dynamic_index_in_dim(all_places, device_index, 1, keepdims=False)
    own_reach = lax.dynamic_index_in_dim(ancestors, device_index, 1, keepdims=False)
    queries = rotate(
        (query_input.astype(jnp.float32) + query_bias).reshape(
            tree_count, row_count, Q_HEADS, HEAD
        ),
        own_places,
        1.0,
    ).astype(jnp.bfloat16)
    tree_length = row_count * devices
    flat_places = all_places.reshape(tree_count, tree_length)
    key_piece = rotate(
        (gathered[:, :, 0].astype(jnp.float32) + key_bias).reshape(
            tree_count, tree_length, KV_HEADS, HEAD
        ),
        flat_places,
        1.0,
    ).astype(jnp.bfloat16)
    value_piece = (
        (gathered[:, :, 1].astype(jnp.float32) + value_bias)
        .astype(jnp.bfloat16)
        .reshape(tree_count, tree_length, KV_HEADS, HEAD)
    )
    reach_flags = (own_reach[0] > 0.5).astype(jnp.int32)
    own_block = jnp.reshape(device_index, (1,)).astype(jnp.int32)
    tall_queries = jnp.transpose(queries.reshape(row_count, Q_HEADS, HEAD), (1, 0, 2)).reshape(
        Q_HEADS * row_count, HEAD
    )
    tall_grads = jnp.transpose(out_grad.reshape(row_count, Q_HEADS, HEAD), (1, 0, 2)).reshape(
        Q_HEADS * row_count, HEAD
    )
    key_stack = key_piece.reshape(devices, row_count, key_width)
    value_stack = value_piece.reshape(devices, row_count, key_width)
    tall_out, log_total = flash_forward(
        reach_flags, own_block, tall_queries, key_stack, value_stack,
        heads=group_size, scale=score_scale,
    )
    row_delta = jnp.sum(
        tall_grads.astype(jnp.float32) * tall_out.astype(jnp.float32), axis=-1, keepdims=True
    )
    tall_dq, grad_pairs = flash_backward(
        reach_flags, own_block, tall_queries, tall_grads, key_stack, value_stack,
        log_total, row_delta, heads=group_size, scale=score_scale,
    )
    out_rows = jnp.transpose(tall_out.reshape(Q_HEADS, row_count, HEAD), (1, 0, 2))
    query_sum = jnp.transpose(tall_dq.reshape(Q_HEADS, row_count, HEAD), (1, 0, 2))
    own_pair = lax.psum_scatter(
        grad_pairs.reshape(tree_count, devices * 2 * row_count, key_width),
        "ctx", scatter_dimension=1, tiled=True,
    ).reshape(tree_count, 2, row_count, key_width).astype(jnp.float32)
    key_full = rotate(
        own_pair[:, 0].reshape(tree_count, row_count, KV_HEADS, HEAD), own_places, -1.0
    ).reshape(tree_count, row_count, key_width)
    value_full = own_pair[:, 1]
    pair_values = grad_pairs.astype(jnp.float32)
    key_total = jnp.sum(
        rotate(pair_values[:, 0].reshape(devices, row_count, KV_HEADS, HEAD), all_places[0], -1.0),
        axis=(0, 1),
    ).reshape(key_width)
    value_total = jnp.sum(pair_values[:, 1], axis=(0, 1))
    query_full = rotate(
        query_sum.reshape(tree_count, row_count, Q_HEADS, HEAD), own_places, -1.0
    ).reshape(tree_count, row_count, query_width)
    attended = out_rows.reshape(tree_count, row_count, query_width)
    query_total = jnp.sum(query_full, axis=(0, 1))
    bias_totals = lax.psum(
        jnp.concatenate([query_total, key_total, value_total]), ("dp", "ctx")
    )
    query_total = bias_totals[:query_width]
    key_total = bias_totals[query_width:query_width + key_width]
    value_total = bias_totals[query_width + key_width:]
    return (attended, query_full, key_full, value_full, query_total, key_total, value_total)


def solution(mesh):
    placed = (
        P("dp", "ctx", None),
        P("dp", "ctx", None),
        P("dp", "ctx", None),
        P("dp", "ctx", None),
        P(),
        P(),
        P(),
        P("dp", None),
    )
    return jax.shard_map(
        body,
        mesh=mesh,
        in_specs=placed,
        out_specs=(
            P("dp", "ctx", None),
            P("dp", "ctx", None),
            P("dp", "ctx", None),
            P("dp", "ctx", None),
            P(),
            P(),
            P(),
        ),
        check_vma=False,
    )
```

```python
import functools
import math

import jax
import jax.numpy as jnp
from jax import lax
from jax.experimental import pallas as pl
from jax.experimental.pallas import tpu as pltpu
from jax.sharding import PartitionSpec as P

Q_HEADS = 64
KV_HEADS = 8
HEAD = 128


LOG_BASE = math.log(1000000.0)
NEG_LARGE = -1e30


def ancestry(parent_list):
    block_count = parent_list.shape[0]
    block_ids = jnp.arange(block_count, dtype=jnp.int32)
    step_matrix = ((parent_list[:, None] == block_ids[None, :]) & (block_ids[:, None] > 0)).astype(
        jnp.float32
    )
    reach = jnp.eye(block_count, dtype=jnp.float32) + step_matrix
    steps = 1
    while steps < block_count:
        reach = jnp.minimum(jnp.dot(reach, reach, precision=lax.Precision.HIGHEST), 1.0)
        steps *= 2
    return reach


def rotate(values, places, direction):
    half_width = values.shape[-1] // 2
    frequency = jnp.exp(
        jnp.arange(half_width, dtype=jnp.float32) * (-2.0 * LOG_BASE / values.shape[-1])
    )
    angles = places[..., None] * frequency
    cosine = jnp.cos(angles)[..., None, :]
    sine_part = direction * jnp.sin(angles)[..., None, :]
    first_half = values[..., :half_width]
    second = values[..., half_width:]
    return jnp.concatenate(
        [first_half * cosine - second * sine_part, second * cosine + first_half * sine_part],
        axis=-1,
    )


def allowed_tiles(reach_values, same_block, row_count):
    row_ids = jnp.arange(row_count, dtype=jnp.int32)
    causal = row_ids[None, :] <= row_ids[:, None]
    return (reach_values[:, None, None] > 0.5) & (jnp.logical_not(same_block) | causal)[None]


def _diagonal_mask(heads, rows):
    row_ids = lax.broadcasted_iota(jnp.int32, (heads, rows, rows), 1)
    col_ids = lax.broadcasted_iota(jnp.int32, (heads, rows, rows), 2)
    return (col_ids <= row_ids).reshape(heads * rows, rows)


def _fwd_kernel(reach_ref, own_ref, q_ref, k_ref, v_ref, o_ref, lse_ref, m_scr, l_scr, acc_scr,
                *, heads, scale):
    block = pl.program_id(1)
    last = pl.num_programs(1) - 1
    rows = k_ref.shape[1]

    @pl.when(block == 0)
    def _():
        m_scr[...] = jnp.full(m_scr.shape, NEG_LARGE, jnp.float32)
        l_scr[...] = jnp.zeros(l_scr.shape, jnp.float32)
        acc_scr[...] = jnp.zeros(acc_scr.shape, jnp.float32)

    def step(masked):
        scores = lax.dot_general(q_ref[...], k_ref[0], (((1,), (1,)), ((), ())),
                                 preferred_element_type=jnp.float32) * scale
        if masked:
            mask = _diagonal_mask(heads, rows)
            scores = jnp.where(mask, scores, NEG_LARGE)
        m_prev = m_scr[...]
        m_new = jnp.maximum(m_prev, jnp.max(scores, axis=-1, keepdims=True))
        weights = jnp.exp(scores - m_new)
        if masked:
            weights = jnp.where(mask, weights, 0.0)
        factor = jnp.exp(m_prev - m_new)
        l_scr[...] = l_scr[...] * factor + jnp.sum(weights, axis=-1, keepdims=True)
        mixed = jnp.dot(weights.astype(jnp.bfloat16), v_ref[0], preferred_element_type=jnp.float32)
        acc_scr[...] = acc_scr[...] * factor + mixed
        m_scr[...] = m_new

    @pl.when(jnp.logical_and(reach_ref[block] > 0, block == own_ref[0]))
    def _():
        step(True)

    @pl.when(jnp.logical_and(reach_ref[block] > 0, block != own_ref[0]))
    def _():
        step(False)

    @pl.when(block == last)
    def _():
        total = l_scr[...]
        o_ref[...] = (acc_scr[...] / total).astype(o_ref.dtype)
        lse_ref[...] = (m_scr[...] + jnp.log(total))[:, :1]


def flash_forward(reach, own, queries, key_stack, value_stack, *, heads, scale, interpret=False):
    blocks, rows, kv_width = key_stack.shape
    head = queries.shape[1]
    groups = kv_width // head
    tall = heads * rows
    kernel = functools.partial(_fwd_kernel, heads=heads, scale=scale)
    grid_spec = pltpu.PrefetchScalarGridSpec(
        num_scalar_prefetch=2,
        grid=(groups, blocks),
        in_specs=[
            pl.BlockSpec((tall, head), lambda g, b, r, o: (g, 0)),
            pl.BlockSpec((1, rows, head), lambda g, b, r, o: (b, 0, g)),
            pl.BlockSpec((1, rows, head), lambda g, b, r, o: (b, 0, g)),
        ],
        out_specs=[
            pl.BlockSpec((tall, head), lambda g, b, r, o: (g, 0)),
            pl.BlockSpec((tall, 1), lambda g, b, r, o: (g, 0)),
        ],
        scratch_shapes=[
            pltpu.VMEM((tall, head), jnp.float32),
            pltpu.VMEM((tall, head), jnp.float32),
            pltpu.VMEM((tall, head), jnp.float32),
        ],
    )
    return pl.pallas_call(
        kernel,
        grid_spec=grid_spec,
        out_shape=[
            jax.ShapeDtypeStruct(queries.shape, jnp.bfloat16),
            jax.ShapeDtypeStruct((queries.shape[0], 1), jnp.float32),
        ],
        compiler_params=pltpu.CompilerParams(dimension_semantics=("arbitrary", "arbitrary")),
        interpret=interpret,
    )(reach, own, queries, key_stack, value_stack)


def _bwd_kernel(reach_ref, own_ref, q_ref, do_ref, k_ref, v_ref, lse_ref, delta_ref,
                dq_ref, dkv_ref, dq_scr, *, heads, scale):
    block = pl.program_id(1)
    last = pl.num_programs(1) - 1
    rows = k_ref.shape[1]

    @pl.when(block == 0)
    def _():
        dq_scr[...] = jnp.zeros(dq_scr.shape, jnp.float32)

    def step(masked):
        query = q_ref[...]
        grad = do_ref[...]
        key = k_ref[0]
        scores = lax.dot_general(query, key, (((1,), (1,)), ((), ())),
                                 preferred_element_type=jnp.float32) * scale
        if masked:
            mask = _diagonal_mask(heads, rows)
            scores = jnp.where(mask, scores, NEG_LARGE)
        probs = jnp.exp(scores - lse_ref[...])
        if masked:
            probs = jnp.where(mask, probs, 0.0)
        grad_probs = lax.dot_general(grad, v_ref[0], (((1,), (1,)), ((), ())),
                                     preferred_element_type=jnp.float32)
        grad_low = (probs * (grad_probs - delta_ref[...])).astype(jnp.bfloat16)
        dq_scr[...] = dq_scr[...] + jnp.dot(grad_low, key, preferred_element_type=jnp.float32) * scale
        key_grad = lax.dot_general(grad_low, query, (((0,), (0,)), ((), ())),
                                   preferred_element_type=jnp.float32) * scale
        value_grad = lax.dot_general(probs.astype(jnp.bfloat16), grad, (((0,), (0,)), ((), ())),
                                     preferred_element_type=jnp.float32)
        dkv_ref[0, 0] = key_grad.astype(dkv_ref.dtype)
        dkv_ref[0, 1] = value_grad.astype(dkv_ref.dtype)

    @pl.when(jnp.logical_and(reach_ref[block] > 0, block == own_ref[0]))
    def _():
        step(True)

    @pl.when(jnp.logical_and(reach_ref[block] > 0, block != own_ref[0]))
    def _():
        step(False)

    @pl.when(reach_ref[block] == 0)
    def _():
        dkv_ref[...] = jnp.zeros(dkv_ref.shape, dkv_ref.dtype)

    @pl.when(block == last)
    def _():
        dq_ref[...] = dq_scr[...]


def flash_backward(reach, own, queries, out_grad, key_stack, value_stack, lse, delta,
                   *, heads, scale, interpret=False):
    blocks, rows, kv_width = key_stack.shape
    head = queries.shape[1]
    groups = kv_width // head
    tall = heads * rows
    kernel = functools.partial(_bwd_kernel, heads=heads, scale=scale)
    grid_spec = pltpu.PrefetchScalarGridSpec(
        num_scalar_prefetch=2,
        grid=(groups, blocks),
        in_specs=[
            pl.BlockSpec((tall, head), lambda g, b, r, o: (g, 0)),
            pl.BlockSpec((tall, head), lambda g, b, r, o: (g, 0)),
            pl.BlockSpec((1, rows, head), lambda g, b, r, o: (b, 0, g)),
            pl.BlockSpec((1, rows, head), lambda g, b, r, o: (b, 0, g)),
            pl.BlockSpec((tall, 1), lambda g, b, r, o: (g, 0)),
            pl.BlockSpec((tall, 1), lambda g, b, r, o: (g, 0)),
        ],
        out_specs=[
            pl.BlockSpec((tall, head), lambda g, b, r, o: (g, 0)),
            pl.BlockSpec((1, 2, rows, head), lambda g, b, r, o: (b, 0, 0, g)),
        ],
        scratch_shapes=[pltpu.VMEM((tall, head), jnp.float32)],
    )
    return pl.pallas_call(
        kernel,
        grid_spec=grid_spec,
        out_shape=[
            jax.ShapeDtypeStruct(queries.shape, jnp.float32),
            jax.ShapeDtypeStruct((blocks, 2, rows, kv_width), jnp.bfloat16),
        ],
        compiler_params=pltpu.CompilerParams(dimension_semantics=("arbitrary", "arbitrary")),
        interpret=interpret,
    )(reach, own, queries, out_grad, key_stack, value_stack, lse, delta)


def body(query_input, key_input, value_input, out_grad, query_bias, key_bias, value_bias, parents):
    tree_count, row_count, query_width = query_input.shape
    key_width = key_input.shape[2]
    score_scale = HEAD ** (-0.5)
    group_size = Q_HEADS // KV_HEADS
    devices = lax.axis_size("ctx")
    device_index = lax.axis_index("ctx")
    raw_pair = jnp.stack([key_input, value_input], axis=2)
    gathered = lax.all_gather(raw_pair, "ctx", axis=1, tiled=True)
    ancestors = jax.vmap(ancestry)(parents)
    block_depth = jnp.sum(ancestors, axis=2) - 1.0
    offsets = jnp.arange(row_count, dtype=jnp.float32)
    all_places = block_depth[:, :, None] * row_count + offsets[None, None, :]
    own_places = lax.dynamic_index_in_dim(all_places, device_index, 1, keepdims=False)
    own_reach = lax.dynamic_index_in_dim(ancestors, device_index, 1, keepdims=False)
    queries = rotate(
        (query_input.astype(jnp.float32) + query_bias).reshape(
            tree_count, row_count, Q_HEADS, HEAD
        ),
        own_places,
        1.0,
    ).astype(jnp.bfloat16)
    tree_length = row_count * devices
    flat_places = all_places.reshape(tree_count, tree_length)
    key_piece = rotate(
        (gathered[:, :, 0].astype(jnp.float32) + key_bias).reshape(
            tree_count, tree_length, KV_HEADS, HEAD
        ),
        flat_places,
        1.0,
    ).astype(jnp.bfloat16)
    value_piece = (
        (gathered[:, :, 1].astype(jnp.float32) + value_bias)
        .astype(jnp.bfloat16)
        .reshape(tree_count, tree_length, KV_HEADS, HEAD)
    )
    reach_flags = (own_reach[0] > 0.5).astype(jnp.int32)
    own_block = jnp.reshape(device_index, (1,)).astype(jnp.int32)
    tall_queries = jnp.transpose(queries.reshape(row_count, Q_HEADS, HEAD), (1, 0, 2)).reshape(
        Q_HEADS * row_count, HEAD
    )
    tall_grads = jnp.transpose(out_grad.reshape(row_count, Q_HEADS, HEAD), (1, 0, 2)).reshape(
        Q_HEADS * row_count, HEAD
    )
    key_stack = key_piece.reshape(devices, row_count, key_width)
    value_stack = value_piece.reshape(devices, row_count, key_width)
    tall_out, log_total = flash_forward(
        reach_flags, own_block, tall_queries, key_stack, value_stack,
        heads=group_size, scale=score_scale,
    )
    row_delta = jnp.sum(
        tall_grads.astype(jnp.float32) * tall_out.astype(jnp.float32), axis=-1, keepdims=True
    )
    tall_dq, grad_pairs = flash_backward(
        reach_flags, own_block, tall_queries, tall_grads, key_stack, value_stack,
        log_total, row_delta, heads=group_size, scale=score_scale,
    )
    out_rows = jnp.transpose(tall_out.reshape(Q_HEADS, row_count, HEAD), (1, 0, 2))
    query_sum = jnp.transpose(tall_dq.reshape(Q_HEADS, row_count, HEAD), (1, 0, 2))
    own_pair = lax.psum_scatter(
        grad_pairs.reshape(tree_count, devices * 2 * row_count, key_width),
        "ctx", scatter_dimension=1, tiled=True,
    ).reshape(tree_count, 2, row_count, key_width).astype(jnp.float32)
    key_full = rotate(
        own_pair[:, 0].reshape(tree_count, row_count, KV_HEADS, HEAD), own_places, -1.0
    ).reshape(tree_count, row_count, key_width)
    value_full = own_pair[:, 1]
    pair_values = grad_pairs.astype(jnp.float32)
    key_total = jnp.sum(
        rotate(pair_values[:, 0].reshape(devices, row_count, KV_HEADS, HEAD), all_places[0], -1.0),
        axis=(0, 1),
    ).reshape(key_width)
    value_total = jnp.sum(pair_values[:, 1], axis=(0, 1))
    query_full = rotate(
        query_sum.reshape(tree_count, row_count, Q_HEADS, HEAD), own_places, -1.0
    ).reshape(tree_count, row_count, query_width)
    attended = out_rows.reshape(tree_count, row_count, query_width)
    query_total = jnp.sum(query_full, axis=(0, 1))
    bias_totals = lax.psum(
        lax.psum(jnp.concatenate([query_total, key_total, value_total]), "ctx"), "dp"
    )
    query_total = bias_totals[:query_width]
    key_total = bias_totals[query_width:query_width + key_width]
    value_total = bias_totals[query_width + key_width:]
    return (attended, query_full, key_full, value_full, query_total, key_total, value_total)


def solution(mesh):
    placed = (
        P("dp", "ctx", None),
        P("dp", "ctx", None),
        P("dp", "ctx", None),
        P("dp", "ctx", None),
        P(),
        P(),
        P(),
        P("dp", None),
    )
    return jax.shard_map(
        body,
        mesh=mesh,
        in_specs=placed,
        out_specs=(
            P("dp", "ctx", None),
            P("dp", "ctx", None),
            P("dp", "ctx", None),
            P("dp", "ctx", None),
            P(),
            P(),
            P(),
        ),
        check_vma=False,
    )
```
